512 devices in a mesh: group: 32 (over y, z_lo, core), expert: 16 (over x, z_hi).
Axes of the slice: x: 4, y: 4, z: 16 (z_hi: 4, z_lo: 4; z = z_hi * 4 + z_lo), core: 2. Of those that a mesh axis runs over, the one named last changes fastest.
Arguments:
- tokens: bfloat16 [65536, 1536], P(('group', 'expert')), may hold values from -6 to 6
- gate_train: float32 [32, 1536, 512], P('expert', 'group'), may hold values from -0.15625 to 0.15625
- up_train: float32 [32, 1536, 512], P('expert', 'group'), may hold values from -0.15625 to 0.15625
- down_train: float32 [32, 512, 1536], P('expert', None, 'group'), may hold values from -0.25 to 0.25
- routes: int32 [65536, 6], P(('group', 'expert')), may hold values from 0 to 31, as said below
- route_scores: float32 [65536, 6], P(('group', 'expert')), may hold values from 0.05 to 1
- live: int32 [65536], P(('group', 'expert')), may hold values from 0 to 1
Outputs:
- moe_out: bfloat16 [65536, 1536], P(('group', 'expert'))
The draws below stay inside these ranges and needn't reach their ends.
Inputs may be any that keep to these rules, and one draw needn't show every extreme that they name: `routes`: each row names 6 different experts; one expert, the same on every device, is named by at least 24 live rows among each device's 128 rows.
All inputs are finite; a program needn't handle non-finite values.
Results may differ from the reference program's by a relative error of at most 0.0075.
Values may be sent and summed in bfloat16 or wider, within the bound.
No kernel may reach another device: no remote copies, remote signals or barrier semaphores. Data moves between devices by JAX's collectives and lax.ppermute only.
A program may use at most 64 MiB of HBM per device.

```python
import math
import jax
import jax.numpy as jnp
from jax import lax

D = 1536
FF = 512
TOP = 6
TOK_DEV = 128
EXPERT_TOTAL = 32
CAP = 24
TOKEN_TOTAL = 65536


def route_helper(key):
    blocks = TOKEN_TOTAL // TOK_DEV
    forced_count = min(TOK_DEV - 2, CAP + CAP // 2 + 1)
    ordering_key, popular_key, boost_key, scoring_key, active_key = jax.random.split(key, 5)
    order_keys = jax.random.randint(ordering_key, (blocks, TOK_DEV), 0, 1 << 20, dtype=jnp.int32) * TOK_DEV + jnp.arange(TOK_DEV, dtype=jnp.int32)[None, :]
    order_rank = jnp.argsort(jnp.argsort(order_keys, axis=1), axis=1)
    forced = (order_rank < forced_count).reshape(TOKEN_TOTAL)
    hot_expert = jax.random.randint(popular_key, (), 0, EXPERT_TOTAL, dtype=jnp.int32)
    expert_ids = jnp.arange(EXPERT_TOTAL, dtype=jnp.int32)
    score_boost = jax.random.randint(boost_key, (EXPERT_TOTAL,), 0, 3, dtype=jnp.int32) * (1 << 18)
    router_scores = jax.random.randint(scoring_key, (TOKEN_TOTAL, EXPERT_TOTAL), 0, 1 << 20, dtype=jnp.int32) + score_boost[None, :]
    router_scores = router_scores + jnp.where(forced[:, None] & (expert_ids[None, :] == hot_expert), 1 << 23, 0).astype(jnp.int32)
    router_scores = router_scores * EXPERT_TOTAL + expert_ids[None, :]
    values, chosen = lax.top_k(router_scores, TOP)
    random_live = jax.random.randint(active_key, (TOKEN_TOTAL,), 0, 4, dtype=jnp.int32) > 0
    live_rows = jnp.where(forced | random_live, 1, 0).astype(jnp.int32)
    return (chosen.astype(jnp.int32), live_rows)


def draw_routes(key, part):
    return route_helper(jax.random.fold_in(key, 4242))[0]


def draw_live(key, part):
    return route_helper(jax.random.fold_in(key, 4242))[1]


def shard_levels(stream_key, extent, cuts, least, high):
    loudness = 1.0
    for dim, blocks in cuts:
        draws = jax.random.uniform(jax.random.fold_in(jax.random.fold_in(stream_key, 6), dim), (blocks,), jnp.float32, least / len(cuts), high / len(cuts))
        loudness = loudness * jnp.repeat(jnp.exp(draws), extent[dim] // blocks).reshape((-1,) + (1,) * (len(extent) - 1 - dim))
    return loudness


def bell_draw(key, shape, spread, bound, pieces=(), kind=jnp.bfloat16):
    result = jax.random.normal(key, shape, jnp.float32) * spread
    if len(pieces) > 0:
        result = shard_levels(key, shape, pieces, -0.22, 0.18) * result
    return jnp.clip(result, min=-bound, max=bound).astype(kind)


def setup_inputs(seed: int = 0) -> dict:
    keys = jax.random.split(jax.random.key(seed), 8)
    tokens = bell_draw(keys[0], (TOKEN_TOTAL, D), 1.0, 6.0, ((0, 512),))
    gate_train = bell_draw(keys[1], (EXPERT_TOTAL, D, FF), D ** -0.5, 0.15625, ((0, 16), (1, 32)), jnp.float32)
    up_train = bell_draw(keys[2], (EXPERT_TOTAL, D, FF), D ** -0.5, 0.15625, ((0, 16), (1, 32)), jnp.float32)
    down_train = bell_draw(keys[3], (EXPERT_TOTAL, FF, D), FF ** -0.5, 0.25, ((0, 16), (2, 32)), jnp.float32)
    routes = draw_routes(jax.random.fold_in(keys[7], 71), 0)
    route_scores = jnp.clip(jnp.exp(math.log(1.0) - 2.9957323 * jax.random.uniform(keys[5], (TOKEN_TOTAL, TOP), jnp.float32) ** shard_levels(keys[5], (TOKEN_TOTAL, TOP), ((0, 512),), -0.2, 0.2)), 0.05, 1.0)
    live = draw_live(jax.random.fold_in(keys[7], 71), 0)
    return {"tokens": tokens, "gate_train": gate_train, "up_train": up_train, "down_train": down_train, "routes": routes, "route_scores": route_scores, "live": live}


def reference(tokens, gate_train, up_train, down_train, routes, route_scores, live):
    gate_up_w = jnp.concatenate([gate_train, up_train], axis=2).astype(jnp.bfloat16)
    down_w = down_train.astype(jnp.bfloat16)
    blocks = TOKEN_TOTAL // TOK_DEV
    route_share = route_scores / jnp.sum(route_scores, axis=1, keepdims=True)
    route_flat = routes.reshape(blocks, TOK_DEV * TOP)
    live_flat = jnp.repeat(live.reshape(blocks, TOK_DEV), TOP, axis=1)
    expert_ids = jnp.arange(EXPERT_TOTAL, dtype=jnp.int32)
    onehot = ((route_flat[:, :, None] == expert_ids[None, None, :]) & (live_flat[:, :, None] > 0)).astype(jnp.int32)
    earlier = jnp.cumsum(onehot, axis=1) - onehot
    slot_index = jnp.sum(earlier * onehot, axis=2)
    kept_mask = (live_flat > 0) & (slot_index < CAP)
    block_ids = jnp.arange(blocks, dtype=jnp.int32)[:, None]
    request_ids = jnp.arange(TOK_DEV * TOP, dtype=jnp.int32)[None, :]
    token_row = (block_ids * TOK_DEV + request_ids // TOP).astype(jnp.int32)
    total_slots = EXPERT_TOTAL * blocks * CAP
    position = jnp.where(kept_mask, route_flat * (blocks * CAP) + block_ids * CAP + slot_index, total_slots).astype(jnp.int32)
    position = position.reshape(-1)
    table_row = jnp.zeros((total_slots,), jnp.int32).at[position].set(token_row.reshape(-1).astype(jnp.int32), mode="drop")
    table_share = jnp.zeros((total_slots,), route_share.dtype).at[position].set(route_share.reshape(-1), mode="drop")
    table_row = table_row.reshape(EXPERT_TOTAL, blocks * CAP)
    table_share = table_share.reshape(EXPERT_TOTAL, blocks * CAP)

    def one_expert(running, inputs):
        weight_gu, weight_down, rows_here, shares_here = inputs
        picked = tokens[rows_here]
        gate_up = jnp.dot(picked, weight_gu, preferred_element_type=jnp.float32)
        hidden = (jax.nn.silu(gate_up[:, :FF]) * gate_up[:, FF:]).astype(jnp.bfloat16)
        expert_rows = jnp.dot(hidden, weight_down, preferred_element_type=jnp.float32).astype(jnp.bfloat16)
        running = running.at[rows_here].add(shares_here[:, None].astype(jnp.float32) * expert_rows.astype(jnp.float32))
        return running, None

    start_acc = jnp.zeros((TOKEN_TOTAL, D), jnp.float32)
    summed, nothing = lax.scan(one_expert, start_acc, (gate_up_w, down_w, table_row, table_share))
    return summed.astype(jnp.bfloat16)
```

```python
import jax
import jax.numpy as jnp
from jax import lax
from jax.sharding import Mesh
from jax.sharding import PartitionSpec as P

AXES = ("y", "zl", "c", "x", "zh")
ROWS = ("y", "zl", "c", "x", "zh")
TOKEN_GROUP = ("x", "zl", "c")


def local(tokens, gate_train, up_train, down_train, routes, route_scores, live):
    hidden_width = gate_train.shape[2]
    tok_dev, model_width = tokens.shape
    top_count = routes.shape[1]
    experts = lax.axis_size(TOKEN_GROUP)
    capacity = tok_dev * top_count // experts
    total_slots = experts * capacity

    slab = jnp.concatenate(
        [gate_train, up_train, jnp.swapaxes(down_train, 1, 2)], axis=2
    ).astype(jnp.bfloat16)
    slab = lax.all_gather(slab, "zh", axis=0, tiled=False)
    n_pairs, local_experts, rows, width = slab.shape
    slab = slab.reshape(n_pairs * local_experts, rows, width)
    slab = lax.all_to_all(slab, ("zl", "c"), split_axis=0, concat_axis=0, tiled=True)
    slab = lax.all_gather(slab, "y", axis=0, tiled=True)
    weights = slab.reshape(model_width, width)
    gate_up_w = weights[:, : 2 * hidden_width]
    down_t = weights[:, 2 * hidden_width :]

    route_share = route_scores / jnp.sum(route_scores, axis=1, keepdims=True)
    flat_route = routes.reshape(-1)
    flat_live = jnp.repeat(live, top_count)
    expert_ids = jnp.arange(experts, dtype=jnp.int32)
    onehot = ((flat_route[:, None] == expert_ids[None, :]) & (flat_live[:, None] > 0)).astype(
        jnp.int32
    )
    earlier = jnp.cumsum(onehot, axis=0) - onehot
    slot_index = jnp.sum(earlier * onehot, axis=1)
    kept_mask = (flat_live > 0) & (slot_index < capacity)
    target = jnp.where(kept_mask, flat_route * capacity + slot_index, total_slots)
    anchor = jnp.arange(tok_dev * top_count, dtype=jnp.int32) // top_count
    source_row = jnp.zeros((total_slots,), jnp.int32).at[target].set(anchor, mode="drop")
    filled = jnp.zeros((total_slots,), jnp.int32).at[target].set(1, mode="drop")
    outgoing = jnp.where(filled[:, None] > 0, tokens[source_row], jnp.zeros((), jnp.bfloat16))
    incoming = lax.all_to_all(outgoing, TOKEN_GROUP, split_axis=0, concat_axis=0, tiled=True)

    gate_up = jnp.dot(incoming, gate_up_w, preferred_element_type=jnp.float32)
    hidden = (jax.nn.silu(gate_up[:, :hidden_width]) * gate_up[:, hidden_width:]).astype(
        jnp.bfloat16
    )
    expert_out = lax.dot_general(
        hidden, down_t, (((1,), (1,)), ((), ())), preferred_element_type=jnp.float32
    )
    expert_rows = expert_out.astype(jnp.bfloat16)
    returned = lax.all_to_all(expert_rows, TOKEN_GROUP, split_axis=0, concat_axis=0, tiled=True)
    picked = returned[jnp.minimum(target, total_slots - 1)]
    weight = jnp.where(kept_mask, route_share.reshape(-1), 0.0)
    combined = jnp.sum(
        picked.reshape(tok_dev, top_count, model_width).astype(jnp.float32)
        * weight.reshape(tok_dev, top_count, 1),
        axis=1,
    )
    return combined.astype(jnp.bfloat16)


def solution(mesh):
    fine = Mesh(mesh.devices.reshape(4, 4, 2, 4, 4), AXES)
    in_specs = (
        P(ROWS, None),
        P(("x", "zh"), ("y", "zl", "c"), None),
        P(("x", "zh"), ("y", "zl", "c"), None),
        P(("x", "zh"), None, ("y", "zl", "c")),
        P(ROWS, None),
        P(ROWS, None),
        P(ROWS),
    )
    out_specs = P(ROWS, None)
    return jax.shard_map(local, mesh=fine, in_specs=in_specs, out_specs=out_specs, check_vma=False)
```

```python
import jax
import jax.numpy as jnp
from jax import lax
from jax.sharding import Mesh
from jax.sharding import PartitionSpec as P

AXES = ("y", "zl", "c", "x", "zh")
ROWS = ("y", "zl", "c", "x", "zh")
TOKEN_GROUP = ("x", "zl", "c")


def local(tokens, gate_train, up_train, down_train, routes, route_scores, live):
    hidden_width = gate_train.shape[2]
    tok_dev, model_width = tokens.shape
    top_count = routes.shape[1]
    experts = lax.axis_size(TOKEN_GROUP)
    capacity = tok_dev * top_count // experts
    total_slots = experts * capacity

    slab = jnp.concatenate(
        [gate_train, up_train, jnp.swapaxes(down_train, 1, 2)], axis=2
    ).astype(jnp.bfloat16)
    slab, tokens, routes, route_scores, live = lax.optimization_barrier(
        (slab, tokens, routes, route_scores, live)
    )
    slab = lax.all_gather(slab, "zh", axis=0, tiled=False)
    n_pairs, local_experts, rows, width = slab.shape
    route_share = route_scores / jnp.sum(route_scores, axis=1, keepdims=True)
    flat_route = routes.reshape(-1)
    flat_live = jnp.repeat(live, top_count)
    expert_ids = jnp.arange(experts, dtype=jnp.int32)
    onehot = ((flat_route[:, None] == expert_ids[None, :]) & (flat_live[:, None] > 0)).astype(
        jnp.int32
    )
    earlier = jnp.cumsum(onehot, axis=0) - onehot
    slot_index = jnp.sum(earlier * onehot, axis=1)
    kept_mask = (flat_live > 0) & (slot_index < capacity)
    target = jnp.where(kept_mask, flat_route * capacity + slot_index, total_slots)
    anchor = jnp.arange(tok_dev * top_count, dtype=jnp.int32) // top_count
    source_row = jnp.zeros((total_slots,), jnp.int32).at[target].set(anchor, mode="drop")
    filled = jnp.zeros((total_slots,), jnp.int32).at[target].set(1, mode="drop")
    outgoing = jnp.where(filled[:, None] > 0, tokens[source_row], jnp.zeros((), jnp.bfloat16))
    incoming = lax.all_to_all(outgoing, TOKEN_GROUP, split_axis=0, concat_axis=0, tiled=True)
    incoming, slab = lax.optimization_barrier((incoming, slab))
    slab = slab.reshape(n_pairs * local_experts, rows, width)
    slab = lax.all_to_all(slab, ("zl", "c"), split_axis=0, concat_axis=0, tiled=True)
    slab = lax.all_gather(slab, "y", axis=0, tiled=True)
    weights = slab.reshape(model_width, width)
    gate_up_w = weights[:, : 2 * hidden_width]
    down_t = weights[:, 2 * hidden_width :]

    gate_up = jnp.dot(incoming, gate_up_w, preferred_element_type=jnp.float32)
    hidden = (jax.nn.silu(gate_up[:, :hidden_width]) * gate_up[:, hidden_width:]).astype(
        jnp.bfloat16
    )
    expert_out = lax.dot_general(
        hidden, down_t, (((1,), (1,)), ((), ())), preferred_element_type=jnp.float32
    )
    expert_rows = expert_out.astype(jnp.bfloat16)
    returned = lax.all_to_all(expert_rows, TOKEN_GROUP, split_axis=0, concat_axis=0, tiled=True)
    picked = returned[jnp.minimum(target, total_slots - 1)]
    weight = jnp.where(kept_mask, route_share.reshape(-1), 0.0)
    combined = jnp.sum(
        picked.reshape(tok_dev, top_count, model_width).astype(jnp.float32)
        * weight.reshape(tok_dev, top_count, 1),
        axis=1,
    )
    return combined.astype(jnp.bfloat16)


def solution(mesh):
    fine = Mesh(mesh.devices.reshape(4, 4, 2, 4, 4), AXES)
    in_specs = (
        P(ROWS, None),
        P(("x", "zh"), ("y", "zl", "c"), None),
        P(("x", "zh"), ("y", "zl", "c"), None),
        P(("x", "zh"), None, ("y", "zl", "c")),
        P(ROWS, None),
        P(ROWS, None),
        P(ROWS),
    )
    out_specs = P(ROWS, None)
    return jax.shard_map(local, mesh=fine, in_specs=in_specs, out_specs=out_specs, check_vma=False)
```

```python
import jax
import jax.numpy as jnp
from jax import lax
from jax.sharding import Mesh
from jax.sharding import PartitionSpec as P

AXES = ("y", "zl", "c", "x", "zh")
ROWS = ("y", "zl", "c", "x", "zh")
TOKEN_GROUP = ("x", "y", "c")


def local(tokens, gate_train, up_train, down_train, routes, route_scores, live):
    hidden_width = gate_train.shape[2]
    tok_dev, model_width = tokens.shape
    top_count = routes.shape[1]
    experts = lax.axis_size(TOKEN_GROUP)
    capacity = tok_dev * top_count // experts
    total_slots = experts * capacity

    slab = jnp.concatenate(
        [gate_train, up_train, jnp.swapaxes(down_train, 1, 2)], axis=2
    ).astype(jnp.bfloat16)
    slab, tokens, routes, route_scores, live = lax.optimization_barrier(
        (slab, tokens, routes, route_scores, live)
    )
    slab = lax.all_gather(slab, "zh", axis=0, tiled=False)
    n_pairs, local_experts, rows, width = slab.shape
    route_share = route_scores / jnp.sum(route_scores, axis=1, keepdims=True)
    flat_route = routes.reshape(-1)
    flat_live = jnp.repeat(live, top_count)
    expert_ids = jnp.arange(experts, dtype=jnp.int32)
    onehot = ((flat_route[:, None] == expert_ids[None, :]) & (flat_live[:, None] > 0)).astype(
        jnp.int32
    )
    earlier = jnp.cumsum(onehot, axis=0) - onehot
    slot_index = jnp.sum(earlier * onehot, axis=1)
    kept_mask = (flat_live > 0) & (slot_index < capacity)
    target = jnp.where(kept_mask, flat_route * capacity + slot_index, total_slots)
    anchor = jnp.arange(tok_dev * top_count, dtype=jnp.int32) // top_count
    source_row = jnp.zeros((total_slots,), jnp.int32).at[target].set(anchor, mode="drop")
    filled = jnp.zeros((total_slots,), jnp.int32).at[target].set(1, mode="drop")
    outgoing = jnp.where(filled[:, None] > 0, tokens[source_row], jnp.zeros((), jnp.bfloat16))
    incoming = lax.all_to_all(outgoing, TOKEN_GROUP, split_axis=0, concat_axis=0, tiled=True)
    incoming, slab = lax.optimization_barrier((incoming, slab))
    slab = slab.reshape(n_pairs * local_experts, rows, width)
    slab = lax.all_to_all(slab, ("y", "c"), split_axis=0, concat_axis=0, tiled=True)
    slab = lax.all_gather(slab, "zl", axis=0, tiled=False)
    zl_size, y_size = slab.shape[0], slab.shape[1] // local_experts
    slab = slab.reshape(zl_size, y_size, local_experts, rows, width)
    weights = jnp.swapaxes(slab, 0, 1).reshape(model_width, width)
    gate_up_w = weights[:, : 2 * hidden_width]
    down_t = weights[:, 2 * hidden_width :]

    gate_up = jnp.dot(incoming, gate_up_w, preferred_element_type=jnp.float32)
    hidden = (jax.nn.silu(gate_up[:, :hidden_width]) * gate_up[:, hidden_width:]).astype(
        jnp.bfloat16
    )
    expert_out = lax.dot_general(
        hidden, down_t, (((1,), (1,)), ((), ())), preferred_element_type=jnp.float32
    )
    expert_rows = expert_out.astype(jnp.bfloat16)
    returned = lax.all_to_all(expert_rows, TOKEN_GROUP, split_axis=0, concat_axis=0, tiled=True)
    picked = returned[jnp.minimum(target, total_slots - 1)]
    weight = jnp.where(kept_mask, route_share.reshape(-1), 0.0)
    combined = jnp.sum(
        picked.reshape(tok_dev, top_count, model_width).astype(jnp.float32)
        * weight.reshape(tok_dev, top_count, 1),
        axis=1,
    )
    return combined.astype(jnp.bfloat16)


def solution(mesh):
    fine = Mesh(mesh.devices.reshape(4, 4, 2, 4, 4), AXES)
    in_specs = (
        P(ROWS, None),
        P(("x", "zh"), ("y", "zl", "c"), None),
        P(("x", "zh"), ("y", "zl", "c"), None),
        P(("x", "zh"), None, ("y", "zl", "c")),
        P(ROWS, None),
        P(ROWS, None),
        P(ROWS),
    )
    out_specs = P(ROWS, None)
    return jax.shard_map(local, mesh=fine, in_specs=in_specs, out_specs=out_specs, check_vma=False)
```

```python
import jax
import jax.numpy as jnp
from jax import lax
from jax.sharding import Mesh
from jax.sharding import PartitionSpec as P

AXES = ("y", "zl", "c", "x", "zh")
ROWS = ("y", "zl", "c", "x", "zh")
TOKEN_GROUP = ("x", "zl", "c")


def local(tokens, gate_train, up_train, down_train, routes, route_scores, live):
    hidden_width = gate_train.shape[2]
    tok_dev, model_width = tokens.shape
    top_count = routes.shape[1]
    experts = lax.axis_size(TOKEN_GROUP)
    capacity = tok_dev * top_count // experts
    total_slots = experts * capacity

    slab = jnp.concatenate(
        [gate_train, up_train, jnp.swapaxes(down_train, 1, 2)], axis=2
    ).astype(jnp.bfloat16)
    slab = lax.all_gather(slab, "zh", axis=0, tiled=False)
    n_pairs, local_experts, rows, width = slab.shape
    slab = slab.reshape(n_pairs * local_experts, rows, width)
    slab = lax.all_to_all(slab, ("zl", "c"), split_axis=0, concat_axis=0, tiled=True)
    slab = lax.all_gather(slab, "y", axis=0, tiled=True)
    weights = slab.reshape(model_width, width)
    gate_up_w = weights[:, : 2 * hidden_width]
    down_t = weights[:, 2 * hidden_width :]

    route_share = route_scores / jnp.sum(route_scores, axis=1, keepdims=True)
    flat_route = routes.reshape(-1)
    flat_live = jnp.repeat(live, top_count)
    expert_ids = jnp.arange(experts, dtype=jnp.int32)
    onehot = ((flat_route[:, None] == expert_ids[None, :]) & (flat_live[:, None] > 0)).astype(
        jnp.int32
    )
    earlier = jnp.cumsum(onehot, axis=0) - onehot
    slot_index = jnp.sum(earlier * onehot, axis=1)
    kept_mask = (flat_live > 0) & (slot_index < capacity)
    target = jnp.where(kept_mask, flat_route * capacity + slot_index, total_slots)
    slot_ids = jnp.arange(total_slots, dtype=jnp.int32)
    picks = target.reshape(tok_dev, top_count)[None, :, :] == slot_ids[:, None, None]
    dispatch = jnp.any(picks, axis=2).astype(jnp.bfloat16)
    outgoing = jnp.dot(dispatch, tokens, preferred_element_type=jnp.float32).astype(jnp.bfloat16)
    incoming = lax.all_to_all(outgoing, TOKEN_GROUP, split_axis=0, concat_axis=0, tiled=True)

    gate_up = jnp.dot(incoming, gate_up_w, preferred_element_type=jnp.float32)
    hidden = (jax.nn.silu(gate_up[:, :hidden_width]) * gate_up[:, hidden_width:]).astype(
        jnp.bfloat16
    )
    expert_out = lax.dot_general(
        hidden, down_t, (((1,), (1,)), ((), ())), preferred_element_type=jnp.float32
    )
    expert_rows = expert_out.astype(jnp.bfloat16)
    returned = lax.all_to_all(expert_rows, TOKEN_GROUP, split_axis=0, concat_axis=0, tiled=True)
    weight = jnp.where(kept_mask, route_share.reshape(-1), 0.0).reshape(tok_dev, top_count)
    combine = jnp.sum(jnp.where(jnp.swapaxes(picks, 0, 1), weight[:, None, :], 0.0), axis=2)
    combine_hi = combine.astype(jnp.bfloat16)
    combine_lo = (combine - combine_hi.astype(jnp.float32)).astype(jnp.bfloat16)
    combined = jnp.dot(combine_hi, returned, preferred_element_type=jnp.float32) + jnp.dot(
        combine_lo, returned, preferred_element_type=jnp.float32
    )
    return combined.astype(jnp.bfloat16)


def solution(mesh):
    fine = Mesh(mesh.devices.reshape(4, 4, 2, 4, 4), AXES)
    in_specs = (
        P(ROWS, None),
        P(("x", "zh"), ("y", "zl", "c"), None),
        P(("x", "zh"), ("y", "zl", "c"), None),
        P(("x", "zh"), None, ("y", "zl", "c")),
        P(ROWS, None),
        P(ROWS, None),
        P(ROWS),
    )
    out_specs = P(ROWS, None)
    return jax.shard_map(local, mesh=fine, in_specs=in_specs, out_specs=out_specs, check_vma=False)
```

```python
import jax
import jax.numpy as jnp
from jax import lax
from jax.sharding import Mesh
from jax.sharding import PartitionSpec as P

AXES = ("y", "zl", "c", "x", "zh")
ROWS = ("y", "zl", "c", "x", "zh")
TOKEN_GROUP = ("x", "zl", "c")


def local(tokens, gate_train, up_train, down_train, routes, route_scores, live):
    hidden_width = gate_train.shape[2]
    tok_dev, model_width = tokens.shape
    top_count = routes.shape[1]
    experts = lax.axis_size(TOKEN_GROUP)
    capacity = tok_dev * top_count // experts
    total_slots = experts * capacity

    slab = jnp.concatenate(
        [gate_train, up_train, jnp.swapaxes(down_train, 1, 2)], axis=2
    ).astype(jnp.bfloat16)
    width = slab.shape[-1]
    zl_size, core_size, zh_size = (lax.axis_size(n) for n in ("zl", "c", "zh"))
    zl_at, core_at, zh_at = (lax.axis_index(n) for n in ("zl", "c", "zh"))
    flat = lambda zl, c, zh: (zl * core_size + c) * zh_size + zh
    received, places = [], []
    for p in range(zl_size):
        for q in range(core_size):
            perm = [
                (flat(j, c, a), flat(a, c ^ q, (j + p) % zh_size))
                for j in range(zl_size)
                for c in range(core_size)
                for a in range(zh_size)
            ]
            piece = jnp.where(core_at == 0, slab[q], slab[1 - q]) if core_size == 2 else slab[q]
            received.append(lax.ppermute(piece, ("zl", "c", "zh"), perm))
            places.append(((zh_at - p) % zl_size) * core_size + (core_at ^ q))
    received = jnp.stack(received)
    order = jnp.argsort(jnp.stack(places))
    slab = jnp.take(received, order, axis=0)
    slab = lax.all_gather(slab, "y", axis=0, tiled=True)
    weights = slab.reshape(model_width, width)
    gate_up_w = weights[:, : 2 * hidden_width]
    down_t = weights[:, 2 * hidden_width :]

    route_share = route_scores / jnp.sum(route_scores, axis=1, keepdims=True)
    flat_route = routes.reshape(-1)
    flat_live = jnp.repeat(live, top_count)
    expert_ids = jnp.arange(experts, dtype=jnp.int32)
    onehot = ((flat_route[:, None] == expert_ids[None, :]) & (flat_live[:, None] > 0)).astype(
        jnp.int32
    )
    earlier = jnp.cumsum(onehot, axis=0) - onehot
    slot_index = jnp.sum(earlier * onehot, axis=1)
    kept_mask = (flat_live > 0) & (slot_index < capacity)
    target = jnp.where(kept_mask, flat_route * capacity + slot_index, total_slots)
    slot_ids = jnp.arange(total_slots, dtype=jnp.int32)
    picks = target.reshape(tok_dev, top_count)[None, :, :] == slot_ids[:, None, None]
    dispatch = jnp.any(picks, axis=2).astype(jnp.bfloat16)
    outgoing = jnp.dot(dispatch, tokens, preferred_element_type=jnp.float32).astype(jnp.bfloat16)
    incoming = lax.all_to_all(outgoing, TOKEN_GROUP, split_axis=0, concat_axis=0, tiled=True)

    gate_up = jnp.dot(incoming, gate_up_w, preferred_element_type=jnp.float32)
    hidden = (jax.nn.silu(gate_up[:, :hidden_width]) * gate_up[:, hidden_width:]).astype(
        jnp.bfloat16
    )
    expert_out = lax.dot_general(
        hidden, down_t, (((1,), (1,)), ((), ())), preferred_element_type=jnp.float32
    )
    expert_rows = expert_out.astype(jnp.bfloat16)
    returned = lax.all_to_all(expert_rows, TOKEN_GROUP, split_axis=0, concat_axis=0, tiled=True)
    weight = jnp.where(kept_mask, route_share.reshape(-1), 0.0).reshape(tok_dev, top_count)
    combine = jnp.sum(jnp.where(jnp.swapaxes(picks, 0, 1), weight[:, None, :], 0.0), axis=2)
    combine_hi = lax.reduce_precision(combine, exponent_bits=8, mantissa_bits=7)
    combine_lo = (combine - combine_hi).astype(jnp.bfloat16)
    combine_hi = combine_hi.astype(jnp.bfloat16)
    combined = jnp.dot(combine_hi, returned, preferred_element_type=jnp.float32) + jnp.dot(
        combine_lo, returned, preferred_element_type=jnp.float32
    )
    return combined.astype(jnp.bfloat16)


def solution(mesh):
    fine = Mesh(mesh.devices.reshape(4, 4, 2, 4, 4), AXES)
    in_specs = (
        P(ROWS, None),
        P(("x", "zh"), ("y", "zl", "c"), None),
        P(("x", "zh"), ("y", "zl", "c"), None),
        P(("x", "zh"), None, ("y", "zl", "c")),
        P(ROWS, None),
        P(ROWS, None),
        P(ROWS),
    )
    out_specs = P(ROWS, None)
    return jax.shard_map(local, mesh=fine, in_specs=in_specs, out_specs=out_specs, check_vma=False)
```

```python
import jax
import jax.numpy as jnp
from jax import lax
from jax.sharding import Mesh
from jax.sharding import PartitionSpec as P

AXES = ("y", "zl", "c", "x", "zh")
ROWS = ("y", "zl", "c", "x", "zh")
TOKEN_GROUP = ("x", "y", "c")


def local(tokens, gate_train, up_train, down_train, routes, route_scores, live):
    hidden_width = gate_train.shape[2]
    tok_dev, model_width = tokens.shape
    top_count = routes.shape[1]
    experts = lax.axis_size(TOKEN_GROUP)
    capacity = tok_dev * top_count // experts
    total_slots = experts * capacity

    slab = jnp.concatenate(
        [gate_train, up_train, jnp.swapaxes(down_train, 1, 2)], axis=2
    ).astype(jnp.bfloat16)
    slab, tokens, routes, route_scores, live = lax.optimization_barrier(
        (slab, tokens, routes, route_scores, live)
    )
    slab = lax.all_gather(slab, "zh", axis=0, tiled=False)
    n_pairs, local_experts, rows, width = slab.shape
    route_share = route_scores / jnp.sum(route_scores, axis=1, keepdims=True)
    flat_route = routes.reshape(-1)
    flat_live = jnp.repeat(live, top_count)
    expert_ids = jnp.arange(experts, dtype=jnp.int32)
    onehot = ((flat_route[:, None] == expert_ids[None, :]) & (flat_live[:, None] > 0)).astype(
        jnp.int32
    )
    earlier = jnp.cumsum(onehot, axis=0) - onehot
    slot_index = jnp.sum(earlier * onehot, axis=1)
    kept_mask = (flat_live > 0) & (slot_index < capacity)
    target = jnp.where(kept_mask, flat_route * capacity + slot_index, total_slots)
    slot_ids = jnp.arange(total_slots, dtype=jnp.int32)
    picks = target.reshape(tok_dev, top_count)[None, :, :] == slot_ids[:, None, None]
    dispatch = jnp.any(picks, axis=2).astype(jnp.bfloat16)
    outgoing = jnp.dot(dispatch, tokens, preferred_element_type=jnp.float32).astype(jnp.bfloat16)
    incoming = lax.all_to_all(outgoing, TOKEN_GROUP, split_axis=0, concat_axis=0, tiled=True)
    incoming, slab = lax.optimization_barrier((incoming, slab))
    slab = slab.reshape(n_pairs * local_experts, rows, width)
    slab = lax.all_to_all(slab, ("y", "c"), split_axis=0, concat_axis=0, tiled=True)
    zl_size, zh_size = lax.axis_size("zl"), lax.axis_size("zh")
    ring = zl_size * zh_size
    index = lambda z: (z % zl_size) * zh_size + z // zl_size
    pairs = lambda k: [(index(z), index((z + k) % ring)) for z in range(ring)]
    shift = lambda v, k: lax.ppermute(v, ("zl", "zh"), pairs(k))
    half = slab.shape[0] // 2
    quarters = [
        slab,
        shift(slab, 1),
        shift(slab, -1),
        jnp.concatenate([shift(slab[:half], 2), shift(slab[half:], -2)]),
    ]
    zl_at = lax.axis_index("zl")
    places = jnp.stack([zl_at, zl_at - 1, zl_at + 1, zl_at + 2]) % zl_size
    slab = jnp.take(jnp.stack(quarters), jnp.argsort(places), axis=0)
    y_size = slab.shape[1] // local_experts
    slab = slab.reshape(zl_size, y_size, local_experts, rows, width)
    weights = jnp.swapaxes(slab, 0, 1).reshape(model_width, width)
    gate_up_w = weights[:, : 2 * hidden_width]
    down_t = weights[:, 2 * hidden_width :]

    gate_up = jnp.dot(incoming, gate_up_w, preferred_element_type=jnp.float32)
    hidden = (jax.nn.silu(gate_up[:, :hidden_width]) * gate_up[:, hidden_width:]).astype(
        jnp.bfloat16
    )
    expert_out = lax.dot_general(
        hidden, down_t, (((1,), (1,)), ((), ())), preferred_element_type=jnp.float32
    )
    expert_rows = expert_out.astype(jnp.bfloat16)
    returned = lax.all_to_all(expert_rows, TOKEN_GROUP, split_axis=0, concat_axis=0, tiled=True)
    weight = jnp.where(kept_mask, route_share.reshape(-1), 0.0).reshape(tok_dev, top_count)
    combine = jnp.sum(jnp.where(jnp.swapaxes(picks, 0, 1), weight[:, None, :], 0.0), axis=2)
    combine_hi = lax.reduce_precision(combine, exponent_bits=8, mantissa_bits=7)
    combine_lo = (combine - combine_hi).astype(jnp.bfloat16)
    combine_hi = combine_hi.astype(jnp.bfloat16)
    combined = jnp.dot(combine_hi, returned, preferred_element_type=jnp.float32) + jnp.dot(
        combine_lo, returned, preferred_element_type=jnp.float32
    )
    return combined.astype(jnp.bfloat16)


def solution(mesh):
    fine = Mesh(mesh.devices.reshape(4, 4, 2, 4, 4), AXES)
    in_specs = (
        P(ROWS, None),
        P(("x", "zh"), ("y", "zl", "c"), None),
        P(("x", "zh"), ("y", "zl", "c"), None),
        P(("x", "zh"), None, ("y", "zl", "c")),
        P(ROWS, None),
        P(ROWS, None),
        P(ROWS),
    )
    out_specs = P(ROWS, None)
    return jax.shard_map(local, mesh=fine, in_specs=in_specs, out_specs=out_specs, check_vma=False)
```

```python
import jax
import jax.numpy as jnp
from jax import lax
from jax.sharding import Mesh
from jax.sharding import PartitionSpec as P

AXES = ("y", "zl", "c", "x", "zh")
ROWS = ("y", "zl", "c", "x", "zh")
TOKEN_GROUP = ("x", "y", "c")


def local(tokens, gate_train, up_train, down_train, routes, route_scores, live):
    hidden_width = gate_train.shape[2]
    tok_dev, model_width = tokens.shape
    top_count = routes.shape[1]
    experts = lax.axis_size(TOKEN_GROUP)
    capacity = tok_dev * top_count // experts
    total_slots = experts * capacity

    parts = 2
    part = hidden_width // parts
    down_t = jnp.swapaxes(down_train, 1, 2)
    slabs = tuple(
        jnp.concatenate(
            [w[:, :, h * part : (h + 1) * part] for w in (gate_train, up_train, down_t)], axis=2
        ).astype(jnp.bfloat16)
        for h in range(parts)
    )
    slabs, tokens, routes, route_scores, live = lax.optimization_barrier(
        (slabs, tokens, routes, route_scores, live)
    )
    slabs = tuple(lax.all_gather(w, "zh", axis=0, tiled=False) for w in slabs)
    n_pairs, local_experts, rows, width = slabs[0].shape
    route_share = route_scores / jnp.sum(route_scores, axis=1, keepdims=True)
    flat_route = routes.reshape(-1)
    flat_live = jnp.repeat(live, top_count)
    expert_ids = jnp.arange(experts, dtype=jnp.int32)
    onehot = ((flat_route[:, None] == expert_ids[None, :]) & (flat_live[:, None] > 0)).astype(
        jnp.int32
    )
    earlier = jnp.cumsum(onehot, axis=0) - onehot
    slot_index = jnp.sum(earlier * onehot, axis=1)
    kept_mask = (flat_live > 0) & (slot_index < capacity)
    target = jnp.where(kept_mask, flat_route * capacity + slot_index, total_slots)
    slot_ids = jnp.arange(total_slots, dtype=jnp.int32)
    picks = target.reshape(tok_dev, top_count)[None, :, :] == slot_ids[:, None, None]
    dispatch = jnp.any(picks, axis=2).astype(jnp.bfloat16)
    outgoing = jnp.dot(dispatch, tokens, preferred_element_type=jnp.float32).astype(jnp.bfloat16)
    incoming = lax.all_to_all(outgoing, TOKEN_GROUP, split_axis=0, concat_axis=0, tiled=True)
    incoming, slabs = lax.optimization_barrier((incoming, slabs))
    zl_size, zh_size = lax.axis_size("zl"), lax.axis_size("zh")
    ring = zl_size * zh_size
    index = lambda z: (z % zl_size) * zh_size + z // zl_size
    pairs = lambda k: [(index(z), index((z + k) % ring)) for z in range(ring)]
    shift = lambda v, k: lax.ppermute(v, ("zl", "zh"), pairs(k))
    zl_at = lax.axis_index("zl")
    places = [zl_at % zl_size, (zl_at - 1) % zl_size, (zl_at + 1) % zl_size, (zl_at + 2) % zl_size]
    weights = []
    for slab in slabs:
        slab = slab.reshape(n_pairs * local_experts, rows, width)
        slab = lax.all_to_all(slab, ("y", "c"), split_axis=0, concat_axis=0, tiled=True)
        half = slab.shape[0] // 2
        quarters = [
            slab,
            shift(slab, 1),
            shift(slab, -1),
            jnp.concatenate([shift(slab[:half], 2), shift(slab[half:], -2)]),
        ]
        y_size = slab.shape[0] // local_experts
        full = jnp.zeros((y_size, zl_size, local_experts, rows, width), jnp.bfloat16)
        for quarter, place in zip(quarters, places):
            quarter = quarter.reshape(y_size, 1, local_experts, rows, width)
            full = lax.dynamic_update_index_in_dim(full, quarter, place, axis=1)
        weights.append(full.reshape(model_width, width))

    expert_out = None
    for w in weights:
        gate_up = jnp.dot(incoming, w[:, : 2 * part], preferred_element_type=jnp.float32)
        hidden = (jax.nn.silu(gate_up[:, :part]) * gate_up[:, part:]).astype(jnp.bfloat16)
        term = lax.dot_general(
            hidden, w[:, 2 * part :], (((1,), (1,)), ((), ())), preferred_element_type=jnp.float32
        )
        expert_out = term if expert_out is None else expert_out + term
    expert_rows = expert_out.astype(jnp.bfloat16)
    returned = lax.all_to_all(expert_rows, TOKEN_GROUP, split_axis=0, concat_axis=0, tiled=True)
    weight = jnp.where(kept_mask, route_share.reshape(-1), 0.0).reshape(tok_dev, top_count)
    combine = jnp.sum(jnp.where(jnp.swapaxes(picks, 0, 1), weight[:, None, :], 0.0), axis=2)
    combine_hi = lax.reduce_precision(combine, exponent_bits=8, mantissa_bits=7)
    combine_lo = (combine - combine_hi).astype(jnp.bfloat16)
    combine_hi = combine_hi.astype(jnp.bfloat16)
    combined = jnp.dot(combine_hi, returned, preferred_element_type=jnp.float32) + jnp.dot(
        combine_lo, returned, preferred_element_type=jnp.float32
    )
    return combined.astype(jnp.bfloat16)


def solution(mesh):
    fine = Mesh(mesh.devices.reshape(4, 4, 2, 4, 4), AXES)
    in_specs = (
        P(ROWS, None),
        P(("x", "zh"), ("y", "zl", "c"), None),
        P(("x", "zh"), ("y", "zl", "c"), None),
        P(("x", "zh"), None, ("y", "zl", "c")),
        P(ROWS, None),
        P(ROWS, None),
        P(ROWS),
    )
    out_specs = P(ROWS, None)
    return jax.shard_map(local, mesh=fine, in_specs=in_specs, out_specs=out_specs, check_vma=False)
```

```python
import jax
import jax.numpy as jnp
from jax import lax
from jax.sharding import Mesh
from jax.sharding import PartitionSpec as P

AXES = ("y", "zl", "c", "x", "zh")
ROWS = ("y", "zl", "c", "x", "zh")
TOKEN_GROUP = ("x", "y", "c")


def local(tokens, gate_train, up_train, down_train, routes, route_scores, live):
    hidden_width = gate_train.shape[2]
    tok_dev, model_width = tokens.shape
    top_count = routes.shape[1]
    experts = lax.axis_size(TOKEN_GROUP)
    capacity = tok_dev * top_count // experts
    total_slots = experts * capacity

    parts = 2
    part = hidden_width // parts
    down_t = jnp.swapaxes(down_train, 1, 2)
    slabs = tuple(
        jnp.concatenate(
            [w[:, :, h * part : (h + 1) * part] for w in (gate_train, up_train, down_t)], axis=2
        ).astype(jnp.bfloat16)
        for h in range(parts)
    )
    slabs, tokens, routes, route_scores, live = lax.optimization_barrier(
        (slabs, tokens, routes, route_scores, live)
    )
    zh_size = lax.axis_size("zh")
    zh_at = lax.axis_index("zh")
    zshift = lambda v, k: lax.ppermute(v, "zh", [(i, (i + k) % zh_size) for i in range(zh_size)])
    local_experts, rows, width = slabs[0].shape
    gathered = []
    for slab in slabs:
        split = rows // 2
        pieces = [
            (0, slab),
            (1, zshift(slab, 1)),
            (-1, zshift(slab, -1)),
            (2, jnp.concatenate([zshift(slab[:, :split], 2), zshift(slab[:, split:], -2)], axis=1)),
        ]
        stack = jnp.zeros((zh_size, local_experts, rows, width), jnp.bfloat16)
        for step, piece in pieces:
            stack = lax.dynamic_update_index_in_dim(stack, piece, (zh_at - step) % zh_size, axis=0)
        gathered.append(stack)
    slabs = tuple(gathered)
    n_pairs = zh_size
    route_share = route_scores / jnp.sum(route_scores, axis=1, keepdims=True)
    flat_route = routes.reshape(-1)
    flat_live = jnp.repeat(live, top_count)
    expert_ids = jnp.arange(experts, dtype=jnp.int32)
    onehot = ((flat_route[:, None] == expert_ids[None, :]) & (flat_live[:, None] > 0)).astype(
        jnp.int32
    )
    earlier = jnp.cumsum(onehot, axis=0) - onehot
    slot_index = jnp.sum(earlier * onehot, axis=1)
    kept_mask = (flat_live > 0) & (slot_index < capacity)
    target = jnp.where(kept_mask, flat_route * capacity + slot_index, total_slots)
    slot_ids = jnp.arange(total_slots, dtype=jnp.int32)
    picks = target.reshape(tok_dev, top_count)[None, :, :] == slot_ids[:, None, None]
    dispatch = jnp.any(picks, axis=2).astype(jnp.bfloat16)
    outgoing = jnp.dot(dispatch, tokens, preferred_element_type=jnp.float32).astype(jnp.bfloat16)
    incoming = lax.all_to_all(outgoing, TOKEN_GROUP, split_axis=0, concat_axis=0, tiled=True)
    incoming, slabs = lax.optimization_barrier((incoming, slabs))
    zl_size = lax.axis_size("zl")
    ring = zl_size * zh_size
    index = lambda z: (z % zl_size) * zh_size + z // zl_size
    pairs = lambda k: [(index(z), index((z + k) % ring)) for z in range(ring)]
    shift = lambda v, k: lax.ppermute(v, ("zl", "zh"), pairs(k))
    zl_at = lax.axis_index("zl")
    places = [zl_at % zl_size, (zl_at - 1) % zl_size, (zl_at + 1) % zl_size, (zl_at + 2) % zl_size]
    weights = []
    for slab in slabs:
        slab = slab.reshape(n_pairs * local_experts, rows, width)
        slab = lax.all_to_all(slab, ("y", "c"), split_axis=0, concat_axis=0, tiled=True)
        half = slab.shape[0] // 2
        quarters = [
            slab,
            shift(slab, 1),
            shift(slab, -1),
            jnp.concatenate([shift(slab[:half], 2), shift(slab[half:], -2)]),
        ]
        y_size = slab.shape[0] // local_experts
        full = jnp.zeros((y_size, zl_size, local_experts, rows, width), jnp.bfloat16)
        for quarter, place in zip(quarters, places):
            quarter = quarter.reshape(y_size, 1, local_experts, rows, width)
            full = lax.dynamic_update_index_in_dim(full, quarter, place, axis=1)
        weights.append(full.reshape(model_width, width))

    expert_out = None
    for w in weights:
        gate_up = jnp.dot(incoming, w[:, : 2 * part], preferred_element_type=jnp.float32)
        hidden = (jax.nn.silu(gate_up[:, :part]) * gate_up[:, part:]).astype(jnp.bfloat16)
        term = lax.dot_general(
            hidden, w[:, 2 * part :], (((1,), (1,)), ((), ())), preferred_element_type=jnp.float32
        )
        expert_out = term if expert_out is None else expert_out + term
    expert_rows = expert_out.astype(jnp.bfloat16)
    returned = lax.all_to_all(expert_rows, TOKEN_GROUP, split_axis=0, concat_axis=0, tiled=True)
    weight = jnp.where(kept_mask, route_share.reshape(-1), 0.0).reshape(tok_dev, top_count)
    combine = jnp.sum(jnp.where(jnp.swapaxes(picks, 0, 1), weight[:, None, :], 0.0), axis=2)
    combine_hi = lax.reduce_precision(combine, exponent_bits=8, mantissa_bits=7)
    combine_lo = (combine - combine_hi).astype(jnp.bfloat16)
    combine_hi = combine_hi.astype(jnp.bfloat16)
    combined = jnp.dot(combine_hi, returned, preferred_element_type=jnp.float32) + jnp.dot(
        combine_lo, returned, preferred_element_type=jnp.float32
    )
    return combined.astype(jnp.bfloat16)


def solution(mesh):
    fine = Mesh(mesh.devices.reshape(4, 4, 2, 4, 4), AXES)
    in_specs = (
        P(ROWS, None),
        P(("x", "zh"), ("y", "zl", "c"), None),
        P(("x", "zh"), ("y", "zl", "c"), None),
        P(("x", "zh"), None, ("y", "zl", "c")),
        P(ROWS, None),
        P(ROWS, None),
        P(ROWS),
    )
    out_specs = P(ROWS, None)
    return jax.shard_map(local, mesh=fine, in_specs=in_specs, out_specs=out_specs, check_vma=False)
```

```python
import jax
import jax.numpy as jnp
from jax import lax
from jax.sharding import Mesh
from jax.sharding import PartitionSpec as P

AXES = ("y", "zl", "c", "x", "zh")
ROWS = ("y", "zl", "c", "x", "zh")
TOKEN_GROUP = ("x", "y", "c")


def local(tokens, gate_train, up_train, down_train, routes, route_scores, live):
    hidden_width = gate_train.shape[2]
    tok_dev, model_width = tokens.shape
    top_count = routes.shape[1]
    experts = lax.axis_size(TOKEN_GROUP)
    capacity = tok_dev * top_count // experts
    total_slots = experts * capacity

    parts = 2
    part = hidden_width // parts
    down_t = jnp.swapaxes(down_train, 1, 2)
    slabs = tuple(
        jnp.concatenate(
            [w[:, :, h * part : (h + 1) * part] for w in (gate_train, up_train, down_t)], axis=2
        ).astype(jnp.bfloat16)
        for h in range(parts)
    )
    slabs, tokens, routes, route_scores, live = lax.optimization_barrier(
        (slabs, tokens, routes, route_scores, live)
    )
    slabs = tuple(lax.all_gather(w, "zh", axis=0, tiled=False) for w in slabs)
    n_pairs, local_experts, rows, width = slabs[0].shape
    slabs, tokens, routes, route_scores, live = lax.optimization_barrier(
        (slabs, tokens, routes, route_scores, live)
    )
    route_share = route_scores / jnp.sum(route_scores, axis=1, keepdims=True)
    flat_route = routes.reshape(-1)
    flat_live = jnp.repeat(live, top_count)
    expert_ids = jnp.arange(experts, dtype=jnp.int32)
    onehot = ((flat_route[:, None] == expert_ids[None, :]) & (flat_live[:, None] > 0)).astype(
        jnp.int32
    )
    earlier = jnp.cumsum(onehot, axis=0) - onehot
    slot_index = jnp.sum(earlier * onehot, axis=1)
    kept_mask = (flat_live > 0) & (slot_index < capacity)
    target = jnp.where(kept_mask, flat_route * capacity + slot_index, total_slots)
    slot_ids = jnp.arange(total_slots, dtype=jnp.int32)
    picks = target.reshape(tok_dev, top_count)[None, :, :] == slot_ids[:, None, None]
    dispatch = jnp.any(picks, axis=2).astype(jnp.bfloat16)
    outgoing = jnp.dot(dispatch, tokens, preferred_element_type=jnp.float32).astype(jnp.bfloat16)
    incoming = lax.all_to_all(outgoing, TOKEN_GROUP, split_axis=0, concat_axis=0, tiled=True)
    zl_size, zh_size = lax.axis_size("zl"), lax.axis_size("zh")
    ring = zl_size * zh_size
    index = lambda z: (z % zl_size) * zh_size + z // zl_size
    pairs = lambda k: [(index(z), index((z + k) % ring)) for z in range(ring)]
    shift = lambda v, k: lax.ppermute(v, ("zl", "zh"), pairs(k))
    zl_at = lax.axis_index("zl")
    places = [zl_at % zl_size, (zl_at - 1) % zl_size, (zl_at + 1) % zl_size, (zl_at + 2) % zl_size]
    weights = []
    for slab in slabs:
        slab = slab.reshape(n_pairs * local_experts, rows, width)
        slab = lax.all_to_all(slab, ("y", "c"), split_axis=0, concat_axis=0, tiled=True)
        half = slab.shape[0] // 2
        quarters = [
            slab,
            shift(slab, 1),
            shift(slab, -1),
            jnp.concatenate([shift(slab[:half], 2), shift(slab[half:], -2)]),
        ]
        y_size = slab.shape[0] // local_experts
        full = jnp.zeros((y_size, zl_size, local_experts, rows, width), jnp.bfloat16)
        for quarter, place in zip(quarters, places):
            quarter = quarter.reshape(y_size, 1, local_experts, rows, width)
            full = lax.dynamic_update_index_in_dim(full, quarter, place, axis=1)
        weights.append(full.reshape(model_width, width))

    expert_out = None
    for w in weights:
        gate_up = jnp.dot(incoming, w[:, : 2 * part], preferred_element_type=jnp.float32)
        hidden = (jax.nn.silu(gate_up[:, :part]) * gate_up[:, part:]).astype(jnp.bfloat16)
        term = lax.dot_general(
            hidden, w[:, 2 * part :], (((1,), (1,)), ((), ())), preferred_element_type=jnp.float32
        )
        expert_out = term if expert_out is None else expert_out + term
    expert_rows = expert_out.astype(jnp.bfloat16)
    returned = lax.all_to_all(expert_rows, TOKEN_GROUP, split_axis=0, concat_axis=0, tiled=True)
    weight = jnp.where(kept_mask, route_share.reshape(-1), 0.0).reshape(tok_dev, top_count)
    combine = jnp.sum(jnp.where(jnp.swapaxes(picks, 0, 1), weight[:, None, :], 0.0), axis=2)
    combine_hi = lax.reduce_precision(combine, exponent_bits=8, mantissa_bits=7)
    combine_lo = (combine - combine_hi).astype(jnp.bfloat16)
    combine_hi = combine_hi.astype(jnp.bfloat16)
    combined = jnp.dot(combine_hi, returned, preferred_element_type=jnp.float32) + jnp.dot(
        combine_lo, returned, preferred_element_type=jnp.float32
    )
    return combined.astype(jnp.bfloat16)


def solution(mesh):
    fine = Mesh(mesh.devices.reshape(4, 4, 2, 4, 4), AXES)
    in_specs = (
        P(ROWS, None),
        P(("x", "zh"), ("y", "zl", "c"), None),
        P(("x", "zh"), ("y", "zl", "c"), None),
        P(("x", "zh"), None, ("y", "zl", "c")),
        P(ROWS, None),
        P(ROWS, None),
        P(ROWS),
    )
    out_specs = P(ROWS, None)
    return jax.shard_map(local, mesh=fine, in_specs=in_specs, out_specs=out_specs, check_vma=False)
```

```python
import jax
import jax.numpy as jnp
from jax import lax
from jax.sharding import Mesh
from jax.sharding import PartitionSpec as P

AXES = ("y", "zl", "c", "x", "zh")
ROWS = ("y", "zl", "c", "x", "zh")
TOKEN_GROUP = ("x", "y", "c")


def local(tokens, gate_train, up_train, down_train, routes, route_scores, live):
    hidden_width = gate_train.shape[2]
    tok_dev, model_width = tokens.shape
    top_count = routes.shape[1]
    experts = lax.axis_size(TOKEN_GROUP)
    capacity = tok_dev * top_count // experts
    total_slots = experts * capacity

    parts = 4
    part = hidden_width // parts
    down_t = jnp.swapaxes(down_train, 1, 2)
    slabs = tuple(
        jnp.concatenate(
            [w[:, :, h * part : (h + 1) * part] for w in (gate_train, up_train, down_t)], axis=2
        ).astype(jnp.bfloat16)
        for h in range(parts)
    )
    slabs, tokens, routes, route_scores, live = lax.optimization_barrier(
        (slabs, tokens, routes, route_scores, live)
    )
    slabs = tuple(lax.all_gather(w, "zh", axis=0, tiled=False) for w in slabs)
    n_pairs, local_experts, rows, width = slabs[0].shape
    route_share = route_scores / jnp.sum(route_scores, axis=1, keepdims=True)
    flat_route = routes.reshape(-1)
    flat_live = jnp.repeat(live, top_count)
    expert_ids = jnp.arange(experts, dtype=jnp.int32)
    onehot = ((flat_route[:, None] == expert_ids[None, :]) & (flat_live[:, None] > 0)).astype(
        jnp.int32
    )
    earlier = jnp.cumsum(onehot, axis=0) - onehot
    slot_index = jnp.sum(earlier * onehot, axis=1)
    kept_mask = (flat_live > 0) & (slot_index < capacity)
    target = jnp.where(kept_mask, flat_route * capacity + slot_index, total_slots)
    slot_ids = jnp.arange(total_slots, dtype=jnp.int32)
    picks = target.reshape(tok_dev, top_count)[None, :, :] == slot_ids[:, None, None]
    dispatch = jnp.any(picks, axis=2).astype(jnp.bfloat16)
    outgoing = jnp.dot(dispatch, tokens, preferred_element_type=jnp.float32).astype(jnp.bfloat16)
    incoming = lax.all_to_all(outgoing, TOKEN_GROUP, split_axis=0, concat_axis=0, tiled=True)
    incoming, slabs = lax.optimization_barrier((incoming, slabs))
    zl_size, zh_size = lax.axis_size("zl"), lax.axis_size("zh")
    ring = zl_size * zh_size
    index = lambda z: (z % zl_size) * zh_size + z // zl_size
    pairs = lambda k: [(index(z), index((z + k) % ring)) for z in range(ring)]
    shift = lambda v, k: lax.ppermute(v, ("zl", "zh"), pairs(k))
    zl_at = lax.axis_index("zl")
    places = [zl_at % zl_size, (zl_at - 1) % zl_size, (zl_at + 1) % zl_size, (zl_at + 2) % zl_size]
    weights = []
    for slab in slabs:
        slab = slab.reshape(n_pairs * local_experts, rows, width)
        slab = lax.all_to_all(slab, ("y", "c"), split_axis=0, concat_axis=0, tiled=True)
        half = slab.shape[0] // 2
        quarters = [
            slab,
            shift(slab, 1),
            shift(slab, -1),
            jnp.concatenate([shift(slab[:half], 2), shift(slab[half:], -2)]),
        ]
        y_size = slab.shape[0] // local_experts
        full = jnp.zeros((y_size, zl_size, local_experts, rows, width), jnp.bfloat16)
        for quarter, place in zip(quarters, places):
            quarter = quarter.reshape(y_size, 1, local_experts, rows, width)
            full = lax.dynamic_update_index_in_dim(full, quarter, place, axis=1)
        weights.append(full.reshape(model_width, width))

    expert_out = None
    for w in weights:
        gate_up = jnp.dot(incoming, w[:, : 2 * part], preferred_element_type=jnp.float32)
        hidden = (jax.nn.silu(gate_up[:, :part]) * gate_up[:, part:]).astype(jnp.bfloat16)
        term = lax.dot_general(
            hidden, w[:, 2 * part :], (((1,), (1,)), ((), ())), preferred_element_type=jnp.float32
        )
        expert_out = term if expert_out is None else expert_out + term
    expert_rows = expert_out.astype(jnp.bfloat16)
    returned = lax.all_to_all(expert_rows, TOKEN_GROUP, split_axis=0, concat_axis=0, tiled=True)
    weight = jnp.where(kept_mask, route_share.reshape(-1), 0.0).reshape(tok_dev, top_count)
    combine = jnp.sum(jnp.where(jnp.swapaxes(picks, 0, 1), weight[:, None, :], 0.0), axis=2)
    combine_hi = lax.reduce_precision(combine, exponent_bits=8, mantissa_bits=7)
    combine_lo = (combine - combine_hi).astype(jnp.bfloat16)
    combine_hi = combine_hi.astype(jnp.bfloat16)
    combined = jnp.dot(combine_hi, returned, preferred_element_type=jnp.float32) + jnp.dot(
        combine_lo, returned, preferred_element_type=jnp.float32
    )
    return combined.astype(jnp.bfloat16)


def solution(mesh):
    fine = Mesh(mesh.devices.reshape(4, 4, 2, 4, 4), AXES)
    in_specs = (
        P(ROWS, None),
        P(("x", "zh"), ("y", "zl", "c"), None),
        P(("x", "zh"), ("y", "zl", "c"), None),
        P(("x", "zh"), None, ("y", "zl", "c")),
        P(ROWS, None),
        P(ROWS, None),
        P(ROWS),
    )
    out_specs = P(ROWS, None)
    return jax.shard_map(local, mesh=fine, in_specs=in_specs, out_specs=out_specs, check_vma=False)
```

```python
import jax
import jax.numpy as jnp
from jax import lax
from jax.sharding import Mesh
from jax.sharding import PartitionSpec as P

AXES = ("y", "zl", "c", "x", "zh")
ROWS = ("y", "zl", "c", "x", "zh")
TOKEN_GROUP = ("x", "y", "c")


def local(tokens, gate_train, up_train, down_train, routes, route_scores, live):
    hidden_width = gate_train.shape[2]
    tok_dev, model_width = tokens.shape
    top_count = routes.shape[1]
    experts = lax.axis_size(TOKEN_GROUP)
    capacity = tok_dev * top_count // experts
    total_slots = experts * capacity

    parts = 2
    part = hidden_width // parts
    down_t = jnp.swapaxes(down_train, 1, 2)
    slabs = tuple(
        jnp.concatenate(
            [w[:, :, h * part : (h + 1) * part] for w in (gate_train, up_train, down_t)], axis=2
        ).astype(jnp.bfloat16)
        for h in range(parts)
    )
    slabs, tokens, routes, route_scores, live = lax.optimization_barrier(
        (slabs, tokens, routes, route_scores, live)
    )
    slabs = tuple(lax.all_gather(w, "zh", axis=0, tiled=False) for w in slabs)
    n_pairs, local_experts, rows, width = slabs[0].shape
    route_share = route_scores / jnp.sum(route_scores, axis=1, keepdims=True)
    flat_route = routes.reshape(-1)
    flat_live = jnp.repeat(live, top_count)
    expert_ids = jnp.arange(experts, dtype=jnp.int32)
    onehot = (flat_route[:, None] == expert_ids[None, :]) & (flat_live[:, None] > 0)
    requests = flat_route.shape[0]
    before = jnp.arange(requests)[None, :] < jnp.arange(requests)[:, None]
    earlier = jnp.dot(
        before.astype(jnp.bfloat16), onehot.astype(jnp.bfloat16), preferred_element_type=jnp.float32
    )
    slot_index = jnp.sum(jnp.where(onehot, earlier, 0.0), axis=1).astype(jnp.int32)
    kept_mask = (flat_live > 0) & (slot_index < capacity)
    target = jnp.where(kept_mask, flat_route * capacity + slot_index, total_slots)
    slot_ids = jnp.arange(total_slots, dtype=jnp.int32)
    picks = target.reshape(tok_dev, top_count)[None, :, :] == slot_ids[:, None, None]
    dispatch = jnp.any(picks, axis=2).astype(jnp.bfloat16)
    outgoing = jnp.dot(dispatch, tokens, preferred_element_type=jnp.float32).astype(jnp.bfloat16)
    incoming = lax.all_to_all(outgoing, TOKEN_GROUP, split_axis=0, concat_axis=0, tiled=True)
    incoming, slabs = lax.optimization_barrier((incoming, slabs))
    zl_size, zh_size = lax.axis_size("zl"), lax.axis_size("zh")
    ring = zl_size * zh_size
    index = lambda z: (z % zl_size) * zh_size + z // zl_size
    pairs = lambda k: [(index(z), index((z + k) % ring)) for z in range(ring)]
    shift = lambda v, k: lax.ppermute(v, ("zl", "zh"), pairs(k))
    zl_at = lax.axis_index("zl")
    places = [zl_at % zl_size, (zl_at - 1) % zl_size, (zl_at + 1) % zl_size, (zl_at + 2) % zl_size]
    weights = []
    for slab in slabs:
        slab = slab.reshape(n_pairs * local_experts, rows, width)
        slab = lax.all_to_all(slab, ("y", "c"), split_axis=0, concat_axis=0, tiled=True)
        half = slab.shape[0] // 2
        quarters = [
            slab,
            shift(slab, 1),
            shift(slab, -1),
            jnp.concatenate([shift(slab[:half], 2), shift(slab[half:], -2)]),
        ]
        y_size = slab.shape[0] // local_experts
        full = jnp.zeros((y_size, zl_size, local_experts, rows, width), jnp.bfloat16)
        for quarter, place in zip(quarters, places):
            quarter = quarter.reshape(y_size, 1, local_experts, rows, width)
            full = lax.dynamic_update_index_in_dim(full, quarter, place, axis=1)
        weights.append(full.reshape(model_width, width))

    expert_out = None
    for w in weights:
        gate_up = jnp.dot(incoming, w[:, : 2 * part], preferred_element_type=jnp.float32)
        hidden = (jax.nn.silu(gate_up[:, :part]) * gate_up[:, part:]).astype(jnp.bfloat16)
        term = lax.dot_general(
            hidden, w[:, 2 * part :], (((1,), (1,)), ((), ())), preferred_element_type=jnp.float32
        )
        expert_out = term if expert_out is None else expert_out + term
    expert_rows = expert_out.astype(jnp.bfloat16)
    returned = lax.all_to_all(expert_rows, TOKEN_GROUP, split_axis=0, concat_axis=0, tiled=True)
    weight = jnp.where(kept_mask, route_share.reshape(-1), 0.0).reshape(tok_dev, top_count)
    combine = jnp.sum(jnp.where(jnp.swapaxes(picks, 0, 1), weight[:, None, :], 0.0), axis=2)
    combine_hi = lax.reduce_precision(combine, exponent_bits=8, mantissa_bits=7)
    combine_lo = (combine - combine_hi).astype(jnp.bfloat16)
    combine_hi = combine_hi.astype(jnp.bfloat16)
    combined = jnp.dot(combine_hi, returned, preferred_element_type=jnp.float32) + jnp.dot(
        combine_lo, returned, preferred_element_type=jnp.float32
    )
    return combined.astype(jnp.bfloat16)


def solution(mesh):
    fine = Mesh(mesh.devices.reshape(4, 4, 2, 4, 4), AXES)
    in_specs = (
        P(ROWS, None),
        P(("x", "zh"), ("y", "zl", "c"), None),
        P(("x", "zh"), ("y", "zl", "c"), None),
        P(("x", "zh"), None, ("y", "zl", "c")),
        P(ROWS, None),
        P(ROWS, None),
        P(ROWS),
    )
    out_specs = P(ROWS, None)
    return jax.shard_map(local, mesh=fine, in_specs=in_specs, out_specs=out_specs, check_vma=False)
```

```python
import jax
import jax.numpy as jnp
from jax import lax
from jax.sharding import Mesh
from jax.sharding import PartitionSpec as P

AXES = ("y", "zl", "c", "x", "zh")
ROWS = ("y", "zl", "c", "x", "zh")
TOKEN_GROUP = ("x", "y", "c")


def local(tokens, gate_train, up_train, down_train, routes, route_scores, live):
    hidden_width = gate_train.shape[2]
    tok_dev, model_width = tokens.shape
    top_count = routes.shape[1]
    experts = lax.axis_size(TOKEN_GROUP)
    capacity = tok_dev * top_count // experts
    total_slots = experts * capacity

    cuts = (0, hidden_width // 4, hidden_width)
    down_t = jnp.swapaxes(down_train, 1, 2)
    slabs = tuple(
        jnp.concatenate([w[:, :, lo:hi] for w in (gate_train, up_train, down_t)], axis=2).astype(
            jnp.bfloat16
        )
        for lo, hi in zip(cuts[:-1], cuts[1:])
    )
    slabs, tokens, routes, route_scores, live = lax.optimization_barrier(
        (slabs, tokens, routes, route_scores, live)
    )
    slabs = tuple(lax.all_gather(w, "zh", axis=0, tiled=False) for w in slabs)
    n_pairs, local_experts, rows = slabs[0].shape[:3]
    route_share = route_scores / jnp.sum(route_scores, axis=1, keepdims=True)
    flat_route = routes.reshape(-1)
    flat_live = jnp.repeat(live, top_count)
    expert_ids = jnp.arange(experts, dtype=jnp.int32)
    onehot = (flat_route[:, None] == expert_ids[None, :]) & (flat_live[:, None] > 0)
    requests = flat_route.shape[0]
    before = jnp.arange(requests)[None, :] < jnp.arange(requests)[:, None]
    earlier = jnp.dot(
        before.astype(jnp.bfloat16), onehot.astype(jnp.bfloat16), preferred_element_type=jnp.float32
    )
    slot_index = jnp.sum(jnp.where(onehot, earlier, 0.0), axis=1).astype(jnp.int32)
    kept_mask = (flat_live > 0) & (slot_index < capacity)
    target = jnp.where(kept_mask, flat_route * capacity + slot_index, total_slots)
    slot_ids = jnp.arange(total_slots, dtype=jnp.int32)
    picks = target.reshape(tok_dev, top_count)[None, :, :] == slot_ids[:, None, None]
    dispatch = jnp.any(picks, axis=2).astype(jnp.bfloat16)
    outgoing = jnp.dot(dispatch, tokens, preferred_element_type=jnp.float32).astype(jnp.bfloat16)
    incoming = lax.all_to_all(outgoing, TOKEN_GROUP, split_axis=0, concat_axis=0, tiled=True)
    incoming, slabs = lax.optimization_barrier((incoming, slabs))
    zl_size, zh_size = lax.axis_size("zl"), lax.axis_size("zh")
    ring = zl_size * zh_size
    index = lambda z: (z % zl_size) * zh_size + z // zl_size
    pairs = lambda k: [(index(z), index((z + k) % ring)) for z in range(ring)]
    shift = lambda v, k: lax.ppermute(v, ("zl", "zh"), pairs(k))
    zl_at = lax.axis_index("zl")
    places = [zl_at % zl_size, (zl_at - 1) % zl_size, (zl_at + 1) % zl_size, (zl_at + 2) % zl_size]
    weights = []
    for slab in slabs:
        width = slab.shape[-1]
        slab = slab.reshape(n_pairs * local_experts, rows, width)
        slab = lax.all_to_all(slab, ("y", "c"), split_axis=0, concat_axis=0, tiled=True)
        half = slab.shape[0] // 2
        quarters = [
            slab,
            shift(slab, 1),
            shift(slab, -1),
            jnp.concatenate([shift(slab[:half], 2), shift(slab[half:], -2)]),
        ]
        y_size = slab.shape[0] // local_experts
        full = jnp.zeros((y_size, zl_size, local_experts, rows, width), jnp.bfloat16)
        for quarter, place in zip(quarters, places):
            quarter = quarter.reshape(y_size, 1, local_experts, rows, width)
            full = lax.dynamic_update_index_in_dim(full, quarter, place, axis=1)
        weights.append(full.reshape(model_width, width))

    expert_out = None
    for w in weights:
        part = w.shape[1] // 3
        gate_up = jnp.dot(incoming, w[:, : 2 * part], preferred_element_type=jnp.float32)
        hidden = (jax.nn.silu(gate_up[:, :part]) * gate_up[:, part:]).astype(jnp.bfloat16)
        term = lax.dot_general(
            hidden, w[:, 2 * part :], (((1,), (1,)), ((), ())), preferred_element_type=jnp.float32
        )
        expert_out = term if expert_out is None else expert_out + term
    expert_rows = expert_out.astype(jnp.bfloat16)
    returned = lax.all_to_all(expert_rows, TOKEN_GROUP, split_axis=0, concat_axis=0, tiled=True)
    weight = jnp.where(kept_mask, route_share.reshape(-1), 0.0).reshape(tok_dev, top_count)
    combine = jnp.sum(jnp.where(jnp.swapaxes(picks, 0, 1), weight[:, None, :], 0.0), axis=2)
    combine_hi = lax.reduce_precision(combine, exponent_bits=8, mantissa_bits=7)
    combine_lo = (combine - combine_hi).astype(jnp.bfloat16)
    combine_hi = combine_hi.astype(jnp.bfloat16)
    combined = jnp.dot(combine_hi, returned, preferred_element_type=jnp.float32) + jnp.dot(
        combine_lo, returned, preferred_element_type=jnp.float32
    )
    return combined.astype(jnp.bfloat16)


def solution(mesh):
    fine = Mesh(mesh.devices.reshape(4, 4, 2, 4, 4), AXES)
    in_specs = (
        P(ROWS, None),
        P(("x", "zh"), ("y", "zl", "c"), None),
        P(("x", "zh"), ("y", "zl", "c"), None),
        P(("x", "zh"), None, ("y", "zl", "c")),
        P(ROWS, None),
        P(ROWS, None),
        P(ROWS),
    )
    out_specs = P(ROWS, None)
    return jax.shard_map(local, mesh=fine, in_specs=in_specs, out_specs=out_specs, check_vma=False)
```

```python
import jax
import jax.numpy as jnp
from jax import lax
from jax.sharding import Mesh
from jax.sharding import PartitionSpec as P

AXES = ("y", "zl", "c", "x", "zh")
ROWS = ("y", "zl", "c", "x", "zh")
TOKEN_GROUP = ("x", "y", "c")


def local(tokens, gate_train, up_train, down_train, routes, route_scores, live):
    hidden_width = gate_train.shape[2]
    tok_dev, model_width = tokens.shape
    top_count = routes.shape[1]
    experts = lax.axis_size(TOKEN_GROUP)
    capacity = tok_dev * top_count // experts
    total_slots = experts * capacity

    parts = 2
    part = hidden_width // parts
    down_t = jnp.swapaxes(down_train, 1, 2)
    slabs = tuple(
        jnp.concatenate(
            [w[:, :, h * part : (h + 1) * part] for w in (gate_train, up_train, down_t)], axis=2
        ).astype(jnp.bfloat16)
        for h in range(parts)
    )
    slabs, tokens, routes, route_scores, live = lax.optimization_barrier(
        (slabs, tokens, routes, route_scores, live)
    )
    first = lax.all_gather(slabs[0], "zh", axis=0, tiled=False)
    n_pairs, local_experts, rows, width = first.shape
    route_share = route_scores / jnp.sum(route_scores, axis=1, keepdims=True)
    flat_route = routes.reshape(-1)
    flat_live = jnp.repeat(live, top_count)
    expert_ids = jnp.arange(experts, dtype=jnp.int32)
    onehot = (flat_route[:, None] == expert_ids[None, :]) & (flat_live[:, None] > 0)
    requests = flat_route.shape[0]
    before = jnp.arange(requests)[None, :] < jnp.arange(requests)[:, None]
    earlier = jnp.dot(
        before.astype(jnp.bfloat16), onehot.astype(jnp.bfloat16), preferred_element_type=jnp.float32
    )
    slot_index = jnp.sum(jnp.where(onehot, earlier, 0.0), axis=1).astype(jnp.int32)
    kept_mask = (flat_live > 0) & (slot_index < capacity)
    target = jnp.where(kept_mask, flat_route * capacity + slot_index, total_slots)
    slot_ids = jnp.arange(total_slots, dtype=jnp.int32)
    picks = target.reshape(tok_dev, top_count)[None, :, :] == slot_ids[:, None, None]
    dispatch = jnp.any(picks, axis=2).astype(jnp.bfloat16)
    outgoing = jnp.dot(dispatch, tokens, preferred_element_type=jnp.float32).astype(jnp.bfloat16)
    incoming = lax.all_to_all(outgoing, TOKEN_GROUP, split_axis=0, concat_axis=0, tiled=True)
    zl_size, zh_size = lax.axis_size("zl"), lax.axis_size("zh")
    ring = zl_size * zh_size
    index = lambda z: (z % zl_size) * zh_size + z // zl_size
    pairs = lambda k: [(index(z), index((z + k) % ring)) for z in range(ring)]
    shift = lambda v, k: lax.ppermute(v, ("zl", "zh"), pairs(k))
    zl_at = lax.axis_index("zl")
    places = [zl_at % zl_size, (zl_at - 1) % zl_size, (zl_at + 1) % zl_size, (zl_at + 2) % zl_size]
    weights = []
    slab = first
    for h in range(len(slabs)):
        if h == len(slabs) - 1:
            incoming, slab = lax.optimization_barrier((incoming, slab))
        slab = slab.reshape(n_pairs * local_experts, rows, width)
        slab = lax.all_to_all(slab, ("y", "c"), split_axis=0, concat_axis=0, tiled=True)
        if h + 1 < len(slabs):
            _, upcoming = lax.optimization_barrier((slab, slabs[h + 1]))
            upcoming = lax.all_gather(upcoming, "zh", axis=0, tiled=False)
        half = slab.shape[0] // 2
        quarters = [
            slab,
            shift(slab, 1),
            shift(slab, -1),
            jnp.concatenate([shift(slab[:half], 2), shift(slab[half:], -2)]),
        ]
        y_size = slab.shape[0] // local_experts
        full = jnp.zeros((y_size, zl_size, local_experts, rows, width), jnp.bfloat16)
        for quarter, place in zip(quarters, places):
            quarter = quarter.reshape(y_size, 1, local_experts, rows, width)
            full = lax.dynamic_update_index_in_dim(full, quarter, place, axis=1)
        weights.append(full.reshape(model_width, width))
        if h + 1 < len(slabs):
            slab = upcoming

    expert_out = None
    for w in weights:
        gate_up = jnp.dot(incoming, w[:, : 2 * part], preferred_element_type=jnp.float32)
        hidden = (jax.nn.silu(gate_up[:, :part]) * gate_up[:, part:]).astype(jnp.bfloat16)
        term = lax.dot_general(
            hidden, w[:, 2 * part :], (((1,), (1,)), ((), ())), preferred_element_type=jnp.float32
        )
        expert_out = term if expert_out is None else expert_out + term
    expert_rows = expert_out.astype(jnp.bfloat16)
    returned = lax.all_to_all(expert_rows, TOKEN_GROUP, split_axis=0, concat_axis=0, tiled=True)
    weight = jnp.where(kept_mask, route_share.reshape(-1), 0.0).reshape(tok_dev, top_count)
    combine = jnp.sum(jnp.where(jnp.swapaxes(picks, 0, 1), weight[:, None, :], 0.0), axis=2)
    combine_hi = lax.reduce_precision(combine, exponent_bits=8, mantissa_bits=7)
    combine_lo = (combine - combine_hi).astype(jnp.bfloat16)
    combine_hi = combine_hi.astype(jnp.bfloat16)
    combined = jnp.dot(combine_hi, returned, preferred_element_type=jnp.float32) + jnp.dot(
        combine_lo, returned, preferred_element_type=jnp.float32
    )
    return combined.astype(jnp.bfloat16)


def solution(mesh):
    fine = Mesh(mesh.devices.reshape(4, 4, 2, 4, 4), AXES)
    in_specs = (
        P(ROWS, None),
        P(("x", "zh"), ("y", "zl", "c"), None),
        P(("x", "zh"), ("y", "zl", "c"), None),
        P(("x", "zh"), None, ("y", "zl", "c")),
        P(ROWS, None),
        P(ROWS, None),
        P(ROWS),
    )
    out_specs = P(ROWS, None)
    return jax.shard_map(local, mesh=fine, in_specs=in_specs, out_specs=out_specs, check_vma=False)
```

```python
import jax
import jax.numpy as jnp
from jax import lax
from jax.sharding import Mesh
from jax.sharding import PartitionSpec as P

AXES = ("y", "zl", "c", "x", "zh")
ROWS = ("y", "zl", "c", "x", "zh")
TOKEN_GROUP = ("y", "x", "c")


def local(tokens, gate_train, up_train, down_train, routes, route_scores, live):
    hidden_width = gate_train.shape[2]
    tok_dev, model_width = tokens.shape
    top_count = routes.shape[1]
    experts = lax.axis_size(TOKEN_GROUP)
    capacity = tok_dev * top_count // experts
    total_slots = experts * capacity

    parts = 2
    part = hidden_width // parts
    down_t = jnp.swapaxes(down_train, 1, 2)
    slabs = tuple(
        jnp.concatenate(
            [w[:, :, h * part : (h + 1) * part] for w in (gate_train, up_train, down_t)], axis=2
        ).astype(jnp.bfloat16)
        for h in range(parts)
    )
    slabs, tokens, routes, route_scores, live = lax.optimization_barrier(
        (slabs, tokens, routes, route_scores, live)
    )
    slabs = tuple(lax.all_gather(w, "zh", axis=0, tiled=False) for w in slabs)
    n_pairs, local_experts, rows, width = slabs[0].shape
    route_share = route_scores / jnp.sum(route_scores, axis=1, keepdims=True)
    flat_route = routes.reshape(-1)
    pair, core = flat_route // 2, flat_route % 2
    x_size = lax.axis_size("x")
    y_size = experts // (2 * x_size)
    flat_route = ((pair % y_size) * x_size + pair // y_size) * 2 + core
    flat_live = jnp.repeat(live, top_count)
    expert_ids = jnp.arange(experts, dtype=jnp.int32)
    onehot = (flat_route[:, None] == expert_ids[None, :]) & (flat_live[:, None] > 0)
    requests = flat_route.shape[0]
    before = jnp.arange(requests)[None, :] < jnp.arange(requests)[:, None]
    earlier = jnp.dot(
        before.astype(jnp.bfloat16), onehot.astype(jnp.bfloat16), preferred_element_type=jnp.float32
    )
    slot_index = jnp.sum(jnp.where(onehot, earlier, 0.0), axis=1).astype(jnp.int32)
    kept_mask = (flat_live > 0) & (slot_index < capacity)
    target = jnp.where(kept_mask, flat_route * capacity + slot_index, total_slots)
    slot_ids = jnp.arange(total_slots, dtype=jnp.int32)
    picks = target.reshape(tok_dev, top_count)[None, :, :] == slot_ids[:, None, None]
    dispatch = jnp.any(picks, axis=2).astype(jnp.bfloat16)
    outgoing = jnp.dot(dispatch, tokens, preferred_element_type=jnp.float32).astype(jnp.bfloat16)
    incoming = lax.all_to_all(outgoing, TOKEN_GROUP, split_axis=0, concat_axis=0, tiled=True)
    incoming, slabs = lax.optimization_barrier((incoming, slabs))
    zl_size, zh_size = lax.axis_size("zl"), lax.axis_size("zh")
    ring = zl_size * zh_size
    index = lambda z: (z % zl_size) * zh_size + z // zl_size
    pairs = lambda k: [(index(z), index((z + k) % ring)) for z in range(ring)]
    shift = lambda v, k: lax.ppermute(v, ("zl", "zh"), pairs(k))
    zl_at = lax.axis_index("zl")
    places = [zl_at % zl_size, (zl_at - 1) % zl_size, (zl_at + 1) % zl_size, (zl_at + 2) % zl_size]
    weights = []
    for slab in slabs:
        slab = slab.reshape(n_pairs * local_experts, rows, width)
        slab = lax.all_to_all(slab, ("y", "c"), split_axis=0, concat_axis=0, tiled=True)
        half = slab.shape[0] // 2
        quarters = [
            slab,
            shift(slab, 1),
            shift(slab, -1),
            jnp.concatenate([shift(slab[:half], 2), shift(slab[half:], -2)]),
        ]
        y_size = slab.shape[0] // local_experts
        full = jnp.zeros((y_size, zl_size, local_experts, rows, width), jnp.bfloat16)
        for quarter, place in zip(quarters, places):
            quarter = quarter.reshape(y_size, 1, local_experts, rows, width)
            full = lax.dynamic_update_index_in_dim(full, quarter, place, axis=1)
        weights.append(full.reshape(model_width, width))

    expert_out = None
    for w in weights:
        gate_up = jnp.dot(incoming, w[:, : 2 * part], preferred_element_type=jnp.float32)
        hidden = (jax.nn.silu(gate_up[:, :part]) * gate_up[:, part:]).astype(jnp.bfloat16)
        term = lax.dot_general(
            hidden, w[:, 2 * part :], (((1,), (1,)), ((), ())), preferred_element_type=jnp.float32
        )
        expert_out = term if expert_out is None else expert_out + term
    expert_rows = expert_out.astype(jnp.bfloat16)
    returned = lax.all_to_all(expert_rows, TOKEN_GROUP, split_axis=0, concat_axis=0, tiled=True)
    weight = jnp.where(kept_mask, route_share.reshape(-1), 0.0).reshape(tok_dev, top_count)
    combine = jnp.sum(jnp.where(jnp.swapaxes(picks, 0, 1), weight[:, None, :], 0.0), axis=2)
    combine_hi = lax.reduce_precision(combine, exponent_bits=8, mantissa_bits=7)
    combine_lo = (combine - combine_hi).astype(jnp.bfloat16)
    combine_hi = combine_hi.astype(jnp.bfloat16)
    combined = jnp.dot(combine_hi, returned, preferred_element_type=jnp.float32) + jnp.dot(
        combine_lo, returned, preferred_element_type=jnp.float32
    )
    return combined.astype(jnp.bfloat16)


def solution(mesh):
    fine = Mesh(mesh.devices.reshape(4, 4, 2, 4, 4), AXES)
    in_specs = (
        P(ROWS, None),
        P(("x", "zh"), ("y", "zl", "c"), None),
        P(("x", "zh"), ("y", "zl", "c"), None),
        P(("x", "zh"), None, ("y", "zl", "c")),
        P(ROWS, None),
        P(ROWS, None),
        P(ROWS),
    )
    out_specs = P(ROWS, None)
    return jax.shard_map(local, mesh=fine, in_specs=in_specs, out_specs=out_specs, check_vma=False)
```

```python
import jax
import jax.numpy as jnp
from jax import lax
from jax.sharding import Mesh
from jax.sharding import PartitionSpec as P

AXES = ("y", "zl", "c", "x", "zh")
ROWS = ("y", "zl", "c", "x", "zh")
TOKEN_GROUP = ("x", "y", "c")


def local(tokens, gate_train, up_train, down_train, routes, route_scores, live):
    hidden_width = gate_train.shape[2]
    tok_dev, model_width = tokens.shape
    top_count = routes.shape[1]
    experts = lax.axis_size(TOKEN_GROUP)
    capacity = tok_dev * top_count // experts
    total_slots = experts * capacity

    parts = 2
    part = hidden_width // parts
    down_t = jnp.swapaxes(down_train, 1, 2)
    slabs = tuple(
        jnp.concatenate(
            [w[:, :, h * part : (h + 1) * part] for w in (gate_train, up_train, down_t)], axis=2
        ).astype(jnp.bfloat16)
        for h in range(parts)
    )
    slabs, tokens, routes, route_scores, live = lax.optimization_barrier(
        (slabs, tokens, routes, route_scores, live)
    )
    slabs = tuple(lax.all_gather(w, "zh", axis=0, tiled=False) for w in slabs)
    n_pairs, local_experts, rows, width = slabs[0].shape
    route_share = route_scores / jnp.sum(route_scores, axis=1, keepdims=True)
    flat_route = routes.reshape(-1)
    flat_live = jnp.repeat(live, top_count)
    expert_ids = jnp.arange(experts, dtype=jnp.int32)
    onehot = (flat_route[:, None] == expert_ids[None, :]) & (flat_live[:, None] > 0)
    requests = flat_route.shape[0]
    before = jnp.arange(requests)[None, :] < jnp.arange(requests)[:, None]
    earlier = jnp.dot(
        before.astype(jnp.bfloat16), onehot.astype(jnp.bfloat16), preferred_element_type=jnp.float32
    )
    slot_index = jnp.sum(jnp.where(onehot, earlier, 0.0), axis=1).astype(jnp.int32)
    kept_mask = (flat_live > 0) & (slot_index < capacity)
    target = jnp.where(kept_mask, flat_route * capacity + slot_index, total_slots)
    slot_ids = jnp.arange(total_slots, dtype=jnp.int32)
    picks = target.reshape(tok_dev, top_count)[None, :, :] == slot_ids[:, None, None]
    dispatch = jnp.any(picks, axis=2).astype(jnp.bfloat16)
    outgoing = jnp.dot(dispatch, tokens, preferred_element_type=jnp.float32).astype(jnp.bfloat16)
    incoming = lax.all_to_all(outgoing, TOKEN_GROUP, split_axis=0, concat_axis=0, tiled=True)
    incoming, slabs = lax.optimization_barrier((incoming, slabs))
    zl_size, zh_size = lax.axis_size("zl"), lax.axis_size("zh")
    ring = zl_size * zh_size
    index = lambda z: (z % zl_size) * zh_size + z // zl_size
    pairs = lambda k: [(index(z), index((z + k) % ring)) for z in range(ring)]
    shift = lambda v, k: lax.ppermute(v, ("zl", "zh"), pairs(k))
    zl_at = lax.axis_index("zl")
    places = [zl_at % zl_size, (zl_at - 1) % zl_size, (zl_at + 1) % zl_size, (zl_at + 2) % zl_size]
    weights = []
    for slab in slabs:
        slab = slab.reshape(n_pairs * local_experts, rows, width)
        slab = lax.all_to_all(slab, ("y", "c"), split_axis=0, concat_axis=0, tiled=True)
        half = slab.shape[0] // 2
        plus, minus = shift(slab, 1), shift(slab, -1)
        quarters = [
            slab,
            plus,
            minus,
            jnp.concatenate([shift(plus[:half], 1), shift(minus[half:], -1)]),
        ]
        y_size = slab.shape[0] // local_experts
        full = jnp.zeros((y_size, zl_size, local_experts, rows, width), jnp.bfloat16)
        for quarter, place in zip(quarters, places):
            quarter = quarter.reshape(y_size, 1, local_experts, rows, width)
            full = lax.dynamic_update_index_in_dim(full, quarter, place, axis=1)
        weights.append(full.reshape(model_width, width))

    expert_out = None
    for w in weights:
        gate_up = jnp.dot(incoming, w[:, : 2 * part], preferred_element_type=jnp.float32)
        hidden = (jax.nn.silu(gate_up[:, :part]) * gate_up[:, part:]).astype(jnp.bfloat16)
        term = lax.dot_general(
            hidden, w[:, 2 * part :], (((1,), (1,)), ((), ())), preferred_element_type=jnp.float32
        )
        expert_out = term if expert_out is None else expert_out + term
    expert_rows = expert_out.astype(jnp.bfloat16)
    returned = lax.all_to_all(expert_rows, TOKEN_GROUP, split_axis=0, concat_axis=0, tiled=True)
    weight = jnp.where(kept_mask, route_share.reshape(-1), 0.0).reshape(tok_dev, top_count)
    combine = jnp.sum(jnp.where(jnp.swapaxes(picks, 0, 1), weight[:, None, :], 0.0), axis=2)
    combine_hi = lax.reduce_precision(combine, exponent_bits=8, mantissa_bits=7)
    combine_lo = (combine - combine_hi).astype(jnp.bfloat16)
    combine_hi = combine_hi.astype(jnp.bfloat16)
    combined = jnp.dot(combine_hi, returned, preferred_element_type=jnp.float32) + jnp.dot(
        combine_lo, returned, preferred_element_type=jnp.float32
    )
    return combined.astype(jnp.bfloat16)


def solution(mesh):
    fine = Mesh(mesh.devices.reshape(4, 4, 2, 4, 4), AXES)
    in_specs = (
        P(ROWS, None),
        P(("x", "zh"), ("y", "zl", "c"), None),
        P(("x", "zh"), ("y", "zl", "c"), None),
        P(("x", "zh"), None, ("y", "zl", "c")),
        P(ROWS, None),
        P(ROWS, None),
        P(ROWS),
    )
    out_specs = P(ROWS, None)
    return jax.shard_map(local, mesh=fine, in_specs=in_specs, out_specs=out_specs, check_vma=False)
```

```python
import jax
import jax.numpy as jnp
from jax import lax
from jax.sharding import Mesh
from jax.sharding import PartitionSpec as P

AXES = ("y", "zl", "c", "x", "zh")
ROWS = ("y", "zl", "c", "x", "zh")
TOKEN_GROUP = ("x", "y", "c")


def local(tokens, gate_train, up_train, down_train, routes, route_scores, live):
    hidden_width = gate_train.shape[2]
    tok_dev, model_width = tokens.shape
    top_count = routes.shape[1]
    experts = lax.axis_size(TOKEN_GROUP)
    capacity = tok_dev * top_count // experts
    total_slots = experts * capacity

    parts = 2
    part = hidden_width // parts
    down_t = jnp.swapaxes(down_train, 1, 2)
    slabs = tuple(
        jnp.concatenate(
            [w[:, :, h * part : (h + 1) * part] for w in (gate_train, up_train, down_t)], axis=2
        ).astype(jnp.bfloat16)
        for h in range(parts)
    )
    slabs, tokens, routes, route_scores, live = lax.optimization_barrier(
        (slabs, tokens, routes, route_scores, live)
    )
    slabs = tuple(lax.all_gather(w, "zh", axis=0, tiled=False) for w in slabs)
    n_pairs, local_experts, rows, width = slabs[0].shape
    route_share = route_scores / jnp.sum(route_scores, axis=1, keepdims=True)
    flat_route = routes.reshape(-1)
    flat_live = jnp.repeat(live, top_count)
    expert_ids = jnp.arange(experts, dtype=jnp.int32)
    onehot = (flat_route[:, None] == expert_ids[None, :]) & (flat_live[:, None] > 0)
    requests = flat_route.shape[0]
    before = jnp.arange(requests)[None, :] < jnp.arange(requests)[:, None]
    earlier = jnp.dot(
        before.astype(jnp.bfloat16), onehot.astype(jnp.bfloat16), preferred_element_type=jnp.float32
    )
    slot_index = jnp.sum(jnp.where(onehot, earlier, 0.0), axis=1).astype(jnp.int32)
    kept_mask = (flat_live > 0) & (slot_index < capacity)
    target = jnp.where(kept_mask, flat_route * capacity + slot_index, total_slots)
    slot_ids = jnp.arange(total_slots, dtype=jnp.int32)
    picks = target.reshape(tok_dev, top_count)[None, :, :] == slot_ids[:, None, None]
    dispatch = jnp.any(picks, axis=2).astype(jnp.bfloat16)
    outgoing = jnp.dot(dispatch, tokens, preferred_element_type=jnp.float32).astype(jnp.bfloat16)
    incoming = lax.all_to_all(outgoing, TOKEN_GROUP, split_axis=0, concat_axis=0, tiled=True)
    incoming, slabs = lax.optimization_barrier((incoming, slabs))
    zl_size, zh_size = lax.axis_size("zl"), lax.axis_size("zh")
    ring = zl_size * zh_size
    index = lambda z: (z % zl_size) * zh_size + z // zl_size
    pairs = lambda k: [(index(z), index((z + k) % ring)) for z in range(ring)]
    shift = lambda v, k: lax.ppermute(v, ("zl", "zh"), pairs(k))
    zl_at = lax.axis_index("zl")
    places = [zl_at % zl_size, (zl_at - 1) % zl_size, (zl_at + 1) % zl_size, (zl_at + 2) % zl_size]
    y_size = experts // (2 * lax.axis_size("x"))

    def assemble(quarters):
        full = jnp.zeros((y_size, zl_size, local_experts, rows, width), jnp.bfloat16)
        for quarter, place in zip(quarters, places):
            quarter = quarter.reshape(y_size, 1, local_experts, rows, width)
            full = lax.dynamic_update_index_in_dim(full, quarter, place, axis=1)
        return full.reshape(model_width, width)

    weights, last = [], None
    for slab in slabs:
        slab = slab.reshape(n_pairs * local_experts, rows, width)
        slab = lax.all_to_all(slab, ("y", "c"), split_axis=0, concat_axis=0, tiled=True)
        count, half = slab.shape[0], slab.shape[0] // 2
        if last is None:
            plus, minus = shift(slab, 1), shift(slab, -1)
        else:
            own, left, right = last
            ahead = shift(jnp.concatenate([slab, left[:half]]), 1)
            behind = shift(jnp.concatenate([slab, right[half:]]), -1)
            plus, minus = ahead[:count], behind[:count]
            weights.append(assemble([own, left, right, jnp.concatenate([ahead[count:], behind[count:]])]))
        last = (slab, plus, minus)
    own, left, right = last
    far = jnp.concatenate([shift(left[:half], 1), shift(right[half:], -1)])
    weights.append(assemble([own, left, right, far]))

    expert_out = None
    for w in weights:
        gate_up = jnp.dot(incoming, w[:, : 2 * part], preferred_element_type=jnp.float32)
        hidden = (jax.nn.silu(gate_up[:, :part]) * gate_up[:, part:]).astype(jnp.bfloat16)
        term = lax.dot_general(
            hidden, w[:, 2 * part :], (((1,), (1,)), ((), ())), preferred_element_type=jnp.float32
        )
        expert_out = term if expert_out is None else expert_out + term
    expert_rows = expert_out.astype(jnp.bfloat16)
    returned = lax.all_to_all(expert_rows, TOKEN_GROUP, split_axis=0, concat_axis=0, tiled=True)
    weight = jnp.where(kept_mask, route_share.reshape(-1), 0.0).reshape(tok_dev, top_count)
    combine = jnp.sum(jnp.where(jnp.swapaxes(picks, 0, 1), weight[:, None, :], 0.0), axis=2)
    combine_hi = lax.reduce_precision(combine, exponent_bits=8, mantissa_bits=7)
    combine_lo = (combine - combine_hi).astype(jnp.bfloat16)
    combine_hi = combine_hi.astype(jnp.bfloat16)
    combined = jnp.dot(combine_hi, returned, preferred_element_type=jnp.float32) + jnp.dot(
        combine_lo, returned, preferred_element_type=jnp.float32
    )
    return combined.astype(jnp.bfloat16)


def solution(mesh):
    fine = Mesh(mesh.devices.reshape(4, 4, 2, 4, 4), AXES)
    in_specs = (
        P(ROWS, None),
        P(("x", "zh"), ("y", "zl", "c"), None),
        P(("x", "zh"), ("y", "zl", "c"), None),
        P(("x", "zh"), None, ("y", "zl", "c")),
        P(ROWS, None),
        P(ROWS, None),
        P(ROWS),
    )
    out_specs = P(ROWS, None)
    return jax.shard_map(local, mesh=fine, in_specs=in_specs, out_specs=out_specs, check_vma=False)
```

```python
import jax
import jax.numpy as jnp
from jax import lax
from jax.sharding import Mesh
from jax.sharding import PartitionSpec as P

AXES = ("y", "zl", "c", "x", "zh")
ROWS = ("y", "zl", "c", "x", "zh")
TOKEN_GROUP = ("x", "y", "c")


def local(tokens, gate_train, up_train, down_train, routes, route_scores, live):
    hidden_width = gate_train.shape[2]
    tok_dev, model_width = tokens.shape
    top_count = routes.shape[1]
    experts = lax.axis_size(TOKEN_GROUP)
    capacity = tok_dev * top_count // experts
    total_slots = experts * capacity

    parts = 2
    part = hidden_width // parts
    down_t = jnp.swapaxes(down_train, 1, 2)
    slabs = tuple(
        jnp.concatenate(
            [w[:, :, h * part : (h + 1) * part] for w in (gate_train, up_train, down_t)], axis=2
        ).astype(jnp.bfloat16)
        for h in range(parts)
    )
    slabs, tokens, routes, route_scores, live = lax.optimization_barrier(
        (slabs, tokens, routes, route_scores, live)
    )
    slabs = tuple(lax.all_gather(w, "zh", axis=0, tiled=False) for w in slabs)
    n_pairs, local_experts, rows, width = slabs[0].shape
    route_share = route_scores / jnp.sum(route_scores, axis=1, keepdims=True)
    flat_route = routes.reshape(-1)
    flat_live = jnp.repeat(live, top_count)
    expert_ids = jnp.arange(experts, dtype=jnp.int32)
    onehot = (flat_route[:, None] == expert_ids[None, :]) & (flat_live[:, None] > 0)
    requests = flat_route.shape[0]
    before = jnp.arange(requests)[None, :] < jnp.arange(requests)[:, None]
    earlier = jnp.dot(
        before.astype(jnp.bfloat16), onehot.astype(jnp.bfloat16), preferred_element_type=jnp.float32
    )
    slot_index = jnp.sum(jnp.where(onehot, earlier, 0.0), axis=1).astype(jnp.int32)
    kept_mask = (flat_live > 0) & (slot_index < capacity)
    target = jnp.where(kept_mask, flat_route * capacity + slot_index, total_slots)
    slot_ids = jnp.arange(total_slots, dtype=jnp.int32)
    picks = target.reshape(tok_dev, top_count)[None, :, :] == slot_ids[:, None, None]
    dispatch = jnp.any(picks, axis=2).astype(jnp.bfloat16)
    outgoing = jnp.dot(dispatch, tokens, preferred_element_type=jnp.float32).astype(jnp.bfloat16)
    incoming = lax.all_to_all(outgoing, TOKEN_GROUP, split_axis=0, concat_axis=0, tiled=True)
    incoming, slabs = lax.optimization_barrier((incoming, slabs))
    zl_size, zh_size = lax.axis_size("zl"), lax.axis_size("zh")
    ring = zl_size * zh_size
    index = lambda z: (z % zl_size) * zh_size + z // zl_size
    pairs = lambda k: [(index(z), index((z + k) % ring)) for z in range(ring)]
    shift = lambda v, k: lax.ppermute(v, ("zl", "zh"), pairs(k))
    zl_at = lax.axis_index("zl")
    places = [zl_at % zl_size, (zl_at - 1) % zl_size, (zl_at + 1) % zl_size, (zl_at + 2) % zl_size]
    weights = []
    for slab in slabs:
        slab = slab.reshape(n_pairs * local_experts, rows, width)
        slab = lax.all_to_all(slab, ("y", "c"), split_axis=0, concat_axis=0, tiled=True)
        half = slab.shape[0] // 2
        plus, minus = shift(slab, 1), shift(slab, -1)
        quarters = [
            slab,
            plus,
            minus,
            jnp.concatenate([shift(plus[:half], 1), shift(minus[half:], -1)]),
        ]
        y_size = slab.shape[0] // local_experts
        quarters = [q.reshape(y_size, local_experts, rows, width) for q in quarters]
        picked = []
        for q in range(zl_size):
            chosen = quarters[0]
            for quarter, place in zip(quarters[1:], places[1:]):
                chosen = jnp.where(place == q, quarter, chosen)
            picked.append(chosen)
        weights.append(jnp.stack(picked, axis=1).reshape(model_width, width))

    expert_out = None
    for w in weights:
        gate_up = jnp.dot(incoming, w[:, : 2 * part], preferred_element_type=jnp.float32)
        hidden = (jax.nn.silu(gate_up[:, :part]) * gate_up[:, part:]).astype(jnp.bfloat16)
        term = lax.dot_general(
            hidden, w[:, 2 * part :], (((1,), (1,)), ((), ())), preferred_element_type=jnp.float32
        )
        expert_out = term if expert_out is None else expert_out + term
    expert_rows = expert_out.astype(jnp.bfloat16)
    returned = lax.all_to_all(expert_rows, TOKEN_GROUP, split_axis=0, concat_axis=0, tiled=True)
    weight = jnp.where(kept_mask, route_share.reshape(-1), 0.0).reshape(tok_dev, top_count)
    combine = jnp.sum(jnp.where(jnp.swapaxes(picks, 0, 1), weight[:, None, :], 0.0), axis=2)
    combine_hi = lax.reduce_precision(combine, exponent_bits=8, mantissa_bits=7)
    combine_lo = (combine - combine_hi).astype(jnp.bfloat16)
    combine_hi = combine_hi.astype(jnp.bfloat16)
    combined = jnp.dot(combine_hi, returned, preferred_element_type=jnp.float32) + jnp.dot(
        combine_lo, returned, preferred_element_type=jnp.float32
    )
    return combined.astype(jnp.bfloat16)


def solution(mesh):
    fine = Mesh(mesh.devices.reshape(4, 4, 2, 4, 4), AXES)
    in_specs = (
        P(ROWS, None),
        P(("x", "zh"), ("y", "zl", "c"), None),
        P(("x", "zh"), ("y", "zl", "c"), None),
        P(("x", "zh"), None, ("y", "zl", "c")),
        P(ROWS, None),
        P(ROWS, None),
        P(ROWS),
    )
    out_specs = P(ROWS, None)
    return jax.shard_map(local, mesh=fine, in_specs=in_specs, out_specs=out_specs, check_vma=False)
```

```python
import jax
import jax.numpy as jnp
from jax import lax
from jax.sharding import Mesh
from jax.sharding import PartitionSpec as P

AXES = ("y", "zl", "c", "x", "zh")
ROWS = ("y", "zl", "c", "x", "zh")
TOKEN_GROUP = ("x", "y", "c")


def local(tokens, gate_train, up_train, down_train, routes, route_scores, live):
    hidden_width = gate_train.shape[2]
    tok_dev, model_width = tokens.shape
    top_count = routes.shape[1]
    experts = lax.axis_size(TOKEN_GROUP)
    capacity = tok_dev * top_count // experts
    total_slots = experts * capacity

    parts = 2
    part = hidden_width // parts
    down_t = jnp.swapaxes(down_train, 1, 2)
    slabs = tuple(
        jnp.concatenate(
            [w[:, :, h * part : (h + 1) * part] for w in (gate_train, up_train, down_t)], axis=2
        ).astype(jnp.bfloat16)
        for h in range(parts)
    )
    slabs, tokens, routes, route_scores, live = lax.optimization_barrier(
        (slabs, tokens, routes, route_scores, live)
    )
    first = lax.all_gather(slabs[0], "zh", axis=0, tiled=False)
    n_pairs, local_experts, rows, width = first.shape
    route_share = route_scores / jnp.sum(route_scores, axis=1, keepdims=True)
    flat_route = routes.reshape(-1)
    flat_live = jnp.repeat(live, top_count)
    expert_ids = jnp.arange(experts, dtype=jnp.int32)
    onehot = (flat_route[:, None] == expert_ids[None, :]) & (flat_live[:, None] > 0)
    requests = flat_route.shape[0]
    before = jnp.arange(requests)[None, :] < jnp.arange(requests)[:, None]
    earlier = jnp.dot(
        before.astype(jnp.bfloat16), onehot.astype(jnp.bfloat16), preferred_element_type=jnp.float32
    )
    slot_index = jnp.sum(jnp.where(onehot, earlier, 0.0), axis=1).astype(jnp.int32)
    kept_mask = (flat_live > 0) & (slot_index < capacity)
    target = jnp.where(kept_mask, flat_route * capacity + slot_index, total_slots)
    slot_ids = jnp.arange(total_slots, dtype=jnp.int32)
    picks = target.reshape(tok_dev, top_count)[None, :, :] == slot_ids[:, None, None]
    dispatch = jnp.any(picks, axis=2).astype(jnp.bfloat16)
    outgoing = jnp.dot(dispatch, tokens, preferred_element_type=jnp.float32).astype(jnp.bfloat16)
    incoming = lax.all_to_all(outgoing, TOKEN_GROUP, split_axis=0, concat_axis=0, tiled=True)
    zl_size, zh_size = lax.axis_size("zl"), lax.axis_size("zh")
    ring = zl_size * zh_size
    index = lambda z: (z % zl_size) * zh_size + z // zl_size
    pairs = lambda k: [(index(z), index((z + k) % ring)) for z in range(ring)]
    shift = lambda v, k: lax.ppermute(v, ("zl", "zh"), pairs(k))
    zl_at = lax.axis_index("zl")
    places = [zl_at % zl_size, (zl_at - 1) % zl_size, (zl_at + 1) % zl_size, (zl_at + 2) % zl_size]
    weights = []
    slab = first
    for h in range(len(slabs)):
        if h == len(slabs) - 1:
            incoming, slab = lax.optimization_barrier((incoming, slab))
        slab = slab.reshape(n_pairs * local_experts, rows, width)
        slab = lax.all_to_all(slab, ("y", "c"), split_axis=0, concat_axis=0, tiled=True)
        if h + 1 < len(slabs):
            _, upcoming = lax.optimization_barrier((slab, slabs[h + 1]))
            upcoming = lax.all_gather(upcoming, "zh", axis=0, tiled=False)
            slab, upcoming = lax.optimization_barrier((slab, upcoming))
        half = slab.shape[0] // 2
        plus, minus = shift(slab, 1), shift(slab, -1)
        quarters = [
            slab,
            plus,
            minus,
            jnp.concatenate([shift(plus[:half], 1), shift(minus[half:], -1)]),
        ]
        y_size = slab.shape[0] // local_experts
        quarters = [q.reshape(y_size, local_experts, rows, width) for q in quarters]
        picked = []
        for q in range(zl_size):
            chosen = quarters[0]
            for quarter, place in zip(quarters[1:], places[1:]):
                chosen = jnp.where(place == q, quarter, chosen)
            picked.append(chosen)
        weights.append(jnp.stack(picked, axis=1).reshape(model_width, width))
        if h + 1 < len(slabs):
            slab = upcoming

    expert_out = None
    for w in weights:
        gate_up = jnp.dot(incoming, w[:, : 2 * part], preferred_element_type=jnp.float32)
        hidden = (jax.nn.silu(gate_up[:, :part]) * gate_up[:, part:]).astype(jnp.bfloat16)
        term = lax.dot_general(
            hidden, w[:, 2 * part :], (((1,), (1,)), ((), ())), preferred_element_type=jnp.float32
        )
        expert_out = term if expert_out is None else expert_out + term
    expert_rows = expert_out.astype(jnp.bfloat16)
    returned = lax.all_to_all(expert_rows, TOKEN_GROUP, split_axis=0, concat_axis=0, tiled=True)
    weight = jnp.where(kept_mask, route_share.reshape(-1), 0.0).reshape(tok_dev, top_count)
    combine = jnp.sum(jnp.where(jnp.swapaxes(picks, 0, 1), weight[:, None, :], 0.0), axis=2)
    combine_hi = lax.reduce_precision(combine, exponent_bits=8, mantissa_bits=7)
    combine_lo = (combine - combine_hi).astype(jnp.bfloat16)
    combine_hi = combine_hi.astype(jnp.bfloat16)
    combined = jnp.dot(combine_hi, returned, preferred_element_type=jnp.float32) + jnp.dot(
        combine_lo, returned, preferred_element_type=jnp.float32
    )
    return combined.astype(jnp.bfloat16)


def solution(mesh):
    fine = Mesh(mesh.devices.reshape(4, 4, 2, 4, 4), AXES)
    in_specs = (
        P(ROWS, None),
        P(("x", "zh"), ("y", "zl", "c"), None),
        P(("x", "zh"), ("y", "zl", "c"), None),
        P(("x", "zh"), None, ("y", "zl", "c")),
        P(ROWS, None),
        P(ROWS, None),
        P(ROWS),
    )
    out_specs = P(ROWS, None)
    return jax.shard_map(local, mesh=fine, in_specs=in_specs, out_specs=out_specs, check_vma=False)
```

```python
import jax
import jax.numpy as jnp
from jax import lax
from jax.sharding import Mesh
from jax.sharding import PartitionSpec as P

AXES = ("y", "zl", "c", "x", "zh")
ROWS = ("y", "zl", "c", "x", "zh")
TOKEN_GROUP = ("x", "y", "c")


def local(tokens, gate_train, up_train, down_train, routes, route_scores, live):
    hidden_width = gate_train.shape[2]
    tok_dev, model_width = tokens.shape
    top_count = routes.shape[1]
    experts = lax.axis_size(TOKEN_GROUP)
    capacity = tok_dev * top_count // experts
    total_slots = experts * capacity

    parts = 2
    part = hidden_width // parts
    down_t = jnp.swapaxes(down_train, 1, 2)
    slabs = tuple(
        jnp.concatenate(
            [w[:, :, h * part : (h + 1) * part] for w in (gate_train, up_train, down_t)], axis=2
        ).astype(jnp.bfloat16)
        for h in range(parts)
    )
    slabs, tokens, routes, route_scores, live = lax.optimization_barrier(
        (slabs, tokens, routes, route_scores, live)
    )
    slabs = tuple(lax.all_gather(w, "zh", axis=0, tiled=False) for w in slabs)
    n_pairs, local_experts, rows, width = slabs[0].shape
    route_share = route_scores / jnp.sum(route_scores, axis=1, keepdims=True)
    flat_route = routes.reshape(-1)
    flat_live = jnp.repeat(live, top_count)
    expert_ids = jnp.arange(experts, dtype=jnp.int32)
    onehot = (flat_route[:, None] == expert_ids[None, :]) & (flat_live[:, None] > 0)
    requests = flat_route.shape[0]
    before = jnp.arange(requests)[None, :] < jnp.arange(requests)[:, None]
    earlier = jnp.dot(
        before.astype(jnp.bfloat16), onehot.astype(jnp.bfloat16), preferred_element_type=jnp.float32
    )
    slot_index = jnp.sum(jnp.where(onehot, earlier, 0.0), axis=1).astype(jnp.int32)
    kept_mask = (flat_live > 0) & (slot_index < capacity)
    target = jnp.where(kept_mask, flat_route * capacity + slot_index, total_slots)
    slot_ids = jnp.arange(total_slots, dtype=jnp.int32)
    picks = target.reshape(tok_dev, top_count)[None, :, :] == slot_ids[:, None, None]
    dispatch = jnp.any(picks, axis=2).astype(jnp.bfloat16)
    outgoing = jnp.dot(dispatch, tokens, preferred_element_type=jnp.float32).astype(jnp.bfloat16)
    incoming = lax.all_to_all(outgoing, TOKEN_GROUP, split_axis=0, concat_axis=0, tiled=True)
    incoming, slabs = lax.optimization_barrier((incoming, slabs))
    zl_size, zh_size = lax.axis_size("zl"), lax.axis_size("zh")
    ring = zl_size * zh_size
    index = lambda z: (z % zl_size) * zh_size + z // zl_size
    pairs = lambda k: [(index(z), index((z + k) % ring)) for z in range(ring)]
    shift = lambda v, k: lax.ppermute(v, ("zl", "zh"), pairs(k))
    zl_at = lax.axis_index("zl")
    places = [zl_at % zl_size, (zl_at - 1) % zl_size, (zl_at + 1) % zl_size, (zl_at + 2) % zl_size]
    weights = []
    for slab in slabs:
        slab = slab.reshape(n_pairs * local_experts, rows, width)
        slab = lax.all_to_all(slab, ("y", "c"), split_axis=0, concat_axis=0, tiled=True)
        halves = slab.reshape(2, slab.shape[0] // 2, rows, width)
        plus, minus = shift(halves, 1), shift(halves, -1)
        quarters = [
            slab,
            plus,
            minus,
            jnp.concatenate([shift(plus[0], 1), shift(minus[1], -1)]),
        ]
        y_size = slab.shape[0] // local_experts
        quarters = [q.reshape(y_size, local_experts, rows, width) for q in quarters]
        picked = []
        for q in range(zl_size):
            chosen = quarters[0]
            for quarter, place in zip(quarters[1:], places[1:]):
                chosen = jnp.where(place == q, quarter, chosen)
            picked.append(chosen)
        weights.append(jnp.stack(picked, axis=1).reshape(model_width, width))

    expert_out = None
    for w in weights:
        gate_up = jnp.dot(incoming, w[:, : 2 * part], preferred_element_type=jnp.float32)
        hidden = (jax.nn.silu(gate_up[:, :part]) * gate_up[:, part:]).astype(jnp.bfloat16)
        term = lax.dot_general(
            hidden, w[:, 2 * part :], (((1,), (1,)), ((), ())), preferred_element_type=jnp.float32
        )
        expert_out = term if expert_out is None else expert_out + term
    expert_rows = expert_out.astype(jnp.bfloat16)
    returned = lax.all_to_all(expert_rows, TOKEN_GROUP, split_axis=0, concat_axis=0, tiled=True)
    weight = jnp.where(kept_mask, route_share.reshape(-1), 0.0).reshape(tok_dev, top_count)
    combine = jnp.sum(jnp.where(jnp.swapaxes(picks, 0, 1), weight[:, None, :], 0.0), axis=2)
    combine_hi = lax.reduce_precision(combine, exponent_bits=8, mantissa_bits=7)
    combine_lo = (combine - combine_hi).astype(jnp.bfloat16)
    combine_hi = combine_hi.astype(jnp.bfloat16)
    combined = jnp.dot(combine_hi, returned, preferred_element_type=jnp.float32) + jnp.dot(
        combine_lo, returned, preferred_element_type=jnp.float32
    )
    return combined.astype(jnp.bfloat16)


def solution(mesh):
    fine = Mesh(mesh.devices.reshape(4, 4, 2, 4, 4), AXES)
    in_specs = (
        P(ROWS, None),
        P(("x", "zh"), ("y", "zl", "c"), None),
        P(("x", "zh"), ("y", "zl", "c"), None),
        P(("x", "zh"), None, ("y", "zl", "c")),
        P(ROWS, None),
        P(ROWS, None),
        P(ROWS),
    )
    out_specs = P(ROWS, None)
    return jax.shard_map(local, mesh=fine, in_specs=in_specs, out_specs=out_specs, check_vma=False)
```

```python
import jax
import jax.numpy as jnp
from jax import lax
from jax.sharding import Mesh
from jax.sharding import PartitionSpec as P

AXES = ("y", "zl", "c", "x", "zh")
ROWS = ("y", "zl", "c", "x", "zh")
TOKEN_GROUP = ("x", "y", "c")


def local(tokens, gate_train, up_train, down_train, routes, route_scores, live):
    hidden_width = gate_train.shape[2]
    tok_dev, model_width = tokens.shape
    top_count = routes.shape[1]
    experts = lax.axis_size(TOKEN_GROUP)
    capacity = tok_dev * top_count // experts
    total_slots = experts * capacity

    parts = 2
    part = hidden_width // parts
    down_t = jnp.swapaxes(down_train, 1, 2)
    slabs = tuple(
        jnp.concatenate(
            [w[:, :, h * part : (h + 1) * part] for w in (gate_train, up_train, down_t)], axis=2
        ).astype(jnp.bfloat16)
        for h in range(parts)
    )
    slabs, tokens, routes, route_scores, live = lax.optimization_barrier(
        (slabs, tokens, routes, route_scores, live)
    )
    slabs = tuple(lax.all_gather(w, "zh", axis=0, tiled=False) for w in slabs)
    n_pairs, local_experts, rows, width = slabs[0].shape
    route_share = route_scores / jnp.sum(route_scores, axis=1, keepdims=True)
    flat_route = routes.reshape(-1)
    flat_live = jnp.repeat(live, top_count)
    expert_ids = jnp.arange(experts, dtype=jnp.int32)
    onehot = (flat_route[:, None] == expert_ids[None, :]) & (flat_live[:, None] > 0)
    requests = flat_route.shape[0]
    before = jnp.arange(requests)[None, :] < jnp.arange(requests)[:, None]
    earlier = jnp.dot(
        before.astype(jnp.bfloat16), onehot.astype(jnp.bfloat16), preferred_element_type=jnp.float32
    )
    slot_index = jnp.sum(jnp.where(onehot, earlier, 0.0), axis=1).astype(jnp.int32)
    kept_mask = (flat_live > 0) & (slot_index < capacity)
    target = jnp.where(kept_mask, flat_route * capacity + slot_index, total_slots)
    slot_ids = jnp.arange(total_slots, dtype=jnp.int32)
    picks = target.reshape(tok_dev, top_count)[None, :, :] == slot_ids[:, None, None]
    dispatch = jnp.any(picks, axis=2).astype(jnp.bfloat16)
    outgoing = jnp.dot(dispatch, tokens, preferred_element_type=jnp.float32).astype(jnp.bfloat16)
    incoming = lax.all_to_all(outgoing, TOKEN_GROUP, split_axis=0, concat_axis=0, tiled=True)
    incoming, slabs = lax.optimization_barrier((incoming, slabs))
    zl_size, zh_size = lax.axis_size("zl"), lax.axis_size("zh")
    ring = zl_size * zh_size
    index = lambda z: (z % zl_size) * zh_size + z // zl_size
    pairs = lambda k: [(index(z), index((z + k) % ring)) for z in range(ring)]
    shift = lambda v, k: lax.ppermute(v, ("zl", "zh"), pairs(k))
    zl_at = lax.axis_index("zl")
    places = [zl_at % zl_size, (zl_at - 1) % zl_size, (zl_at + 1) % zl_size, (zl_at + 2) % zl_size]
    weights = []
    for slab in slabs:
        slab = slab.reshape(n_pairs * local_experts, rows, width)
        slab = lax.all_to_all(slab, ("y", "c"), split_axis=0, concat_axis=0, tiled=True)
        halves = slab.reshape(2, slab.shape[0] // 2, rows, width)
        plus, minus = shift(halves, 1), shift(halves, -1)
        quarters = [
            slab,
            plus,
            minus,
            jnp.concatenate([shift(plus[0], 1), shift(minus[1], -1)]),
        ]
        y_size = slab.shape[0] // local_experts
        quarters = [q.reshape(y_size, local_experts, rows, width) for q in quarters]
        picked = []
        for q in range(zl_size):
            chosen = quarters[0]
            for quarter, place in zip(quarters[1:], places[1:]):
                chosen = jnp.where(place == q, quarter, chosen)
            picked.append(chosen)
        weights.append(jnp.stack(picked, axis=1).reshape(model_width, width))

    expert_out = None
    for w in weights:
        gate_up = jnp.dot(incoming, w[:, : 2 * part], preferred_element_type=jnp.float32)
        hidden = (jax.nn.silu(gate_up[:, :part]) * gate_up[:, part:]).astype(jnp.bfloat16)
        term = lax.dot_general(
            hidden, w[:, 2 * part :], (((1,), (1,)), ((), ())), preferred_element_type=jnp.float32
        )
        expert_out = term if expert_out is None else expert_out + term
    expert_rows = expert_out.astype(jnp.bfloat16)
    returned = lax.all_to_all(expert_rows, TOKEN_GROUP, split_axis=0, concat_axis=0, tiled=True)
    weight = jnp.where(kept_mask, route_share.reshape(-1), 0.0).reshape(tok_dev, top_count)
    combine = jnp.sum(jnp.where(jnp.swapaxes(picks, 0, 1), weight[:, None, :], 0.0), axis=2)
    combine_hi = lax.reduce_precision(combine, exponent_bits=8, mantissa_bits=7)
    combine_lo = (combine - combine_hi).astype(jnp.bfloat16)
    combine_hi = combine_hi.astype(jnp.bfloat16)
    both = jnp.dot(
        jnp.concatenate([combine_hi, combine_lo]), returned, preferred_element_type=jnp.float32
    )
    combined = both[:tok_dev] + both[tok_dev:]
    return combined.astype(jnp.bfloat16)


def solution(mesh):
    fine = Mesh(mesh.devices.reshape(4, 4, 2, 4, 4), AXES)
    in_specs = (
        P(ROWS, None),
        P(("x", "zh"), ("y", "zl", "c"), None),
        P(("x", "zh"), ("y", "zl", "c"), None),
        P(("x", "zh"), None, ("y", "zl", "c")),
        P(ROWS, None),
        P(ROWS, None),
        P(ROWS),
    )
    out_specs = P(ROWS, None)
    return jax.shard_map(local, mesh=fine, in_specs=in_specs, out_specs=out_specs, check_vma=False)
```
